32 devices in a mesh: gx: 8 (over z, y), gy: 4 (over x, core).
Axes of the slice: x: 2, y: 2, z: 4, core: 2. Of those that a mesh axis runs over, the one named last changes fastest.
Arguments:
- start_panel: float32 [16, 64, 128, 128], P(None, 'gx', 'gy'), may hold values from -6 to 6
- ocean_mask: int32 [64, 128, 128], P('gx', 'gy'), may hold values from 0 to 1, as said below
- conduct_x: float32 [64, 128, 128], P('gx', 'gy'), may hold values from 0.3 to 3
- conduct_y: float32 [64, 128, 128], P('gx', 'gy'), may hold values from 0.3 to 3
- conduct_z: float32 [64, 128, 128], P('gx', 'gy'), may hold values from 0.3 to 3
- diag_shift: float32 [64, 128, 128], P('gx', 'gy'), may hold values from 0.5 to 2
Outputs:
- basis_out: float32 [16, 64, 128, 128], P(None, 'gx', 'gy')
- ritz_residual: float32 [16, 64, 128, 128], P(None, 'gx', 'gy')
The draws below stay inside these ranges and needn't reach their ends.
Inputs may be any that keep to these rules, and one draw needn't show every extreme that they name: `ocean_mask`: 1 marks an ocean cell; the share of ocean cells falls along the first dimension from about 0.9 to about 0.2.
All inputs are finite; a program needn't handle non-finite values.
Results may differ from the reference program's by a relative error of at most 0.0003.
Values sent between devices are 32-bit elements; how exact they have to be, the bound alone decides.
No kernel may reach another device: no remote copies, remote signals or barrier semaphores. Data moves between devices by JAX's collectives and lax.ppermute only.
A program may use at most 64 MiB of HBM per device.

```python
import math
import jax
import jax.numpy as jnp
from jax import lax

PANEL = 16
FILTER_STEPS = 2
NX = 64
NY = 128
NZ = 128


def draw_ocean_mask(key, part):
    position = lax.broadcasted_iota(jnp.int32, (NX, NY, NZ), 0)
    threshold = 100 + 700 * position // NX
    ticket = jax.random.randint(key, (NX, NY, NZ), 0, 1000)
    return (ticket >= threshold).astype(jnp.int32)


def steps_of(rng, extent, split, smallest, largest):
    def one(dim, shards_of):
        draws = jax.random.uniform(jax.random.fold_in(jax.random.fold_in(rng, 6), dim), (shards_of,), jnp.float32, smallest / len(split), largest / len(split))
        return jnp.repeat(jnp.exp(draws), extent[dim] // shards_of).reshape((-1,) + (1,) * (len(extent) - dim - 1))

    factor_of = one(*split[0])
    for cut in split[1:]:
        factor_of = factor_of * one(*cut)
    return factor_of


def gaussian(stream_key, shape, width, bound, pieces=(), kind=jnp.bfloat16):
    loudness = steps_of(stream_key, shape, pieces, -0.22, 0.18) if pieces else 1.0
    values = jax.random.normal(stream_key, shape, jnp.float32) * width * loudness
    return jnp.minimum(jnp.maximum(values, -bound), bound).astype(kind)


def setup_inputs(seed: int = 0) -> dict:
    key_of = jax.random.split(jax.random.key(seed), 7)
    return {
        "start_panel": gaussian(key_of[0], (PANEL, NX, NY, NZ), 1.0, 6.0, ((1, 8), (2, 4)), jnp.float32),
        "ocean_mask": draw_ocean_mask(jax.random.fold_in(key_of[6], 71), 0),
        "conduct_x": jnp.clip(jnp.exp(math.log(3.0) - 2.3025851 * jax.random.uniform(key_of[2], (NX, NY, NZ), jnp.float32) ** steps_of(key_of[2], (NX, NY, NZ), ((0, 8), (1, 4)), -0.2, 0.2)), 0.3, 3.0),
        "conduct_y": jnp.clip(jnp.exp(math.log(3.0) - 2.3025851 * jax.random.uniform(key_of[3], (NX, NY, NZ), jnp.float32) ** steps_of(key_of[3], (NX, NY, NZ), ((0, 8), (1, 4)), -0.2, 0.2)), 0.3, 3.0),
        "conduct_z": jnp.clip(jnp.exp(math.log(3.0) - 2.3025851 * jax.random.uniform(key_of[4], (NX, NY, NZ), jnp.float32) ** steps_of(key_of[4], (NX, NY, NZ), ((0, 8), (1, 4)), -0.2, 0.2)), 0.3, 3.0),
        "diag_shift": jnp.clip(jnp.exp(math.log(2.0) - 1.3862944 * jax.random.uniform(key_of[5], (NX, NY, NZ), jnp.float32) ** steps_of(key_of[5], (NX, NY, NZ), ((0, 8), (1, 4)), -0.2, 0.2)), 0.5, 2.0),
    }


FILTER_CENTRE = 22.0
FILTER_HALF = 18.0
FILTER_NORM = 2.0 * (22.0 / 18.0) * (22.0 / 18.0) - 1.0

def stencil(values, fields):
    wet_mask = fields[0]
    along_x = fields[1]
    along_y = fields[2]
    along_z = fields[3]
    diag_term = fields[4]
    inner_wet = wet_mask[1:-1, 1:-1]
    face_x = along_x[:-1, 1:-1] * wet_mask[:-1, 1:-1] * wet_mask[1:, 1:-1]
    flow_x = face_x * (values[..., 1:, 1:-1, :] - values[..., :-1, 1:-1, :])
    face_y = along_y[1:-1, :-1] * wet_mask[1:-1, :-1] * wet_mask[1:-1, 1:]
    flow_y = face_y * (values[..., 1:-1, 1:, :] - values[..., 1:-1, :-1, :])
    centre = values[..., 1:-1, 1:-1, :]
    face_z = along_z[1:-1, 1:-1, :-1] * inner_wet[:, :, :-1] * inner_wet[:, :, 1:]
    flow_z = face_z * (centre[..., 1:] - centre[..., :-1])
    edges = [(0, 0)] * (centre.ndim - 1)
    net_z = jnp.pad(flow_z, edges + [(1, 0)]) - jnp.pad(flow_z, edges + [(0, 1)])
    net_x = flow_x[..., :-1, :, :] - flow_x[..., 1:, :, :]
    net_y = flow_y[..., :-1, :] - flow_y[..., 1:, :]
    return inner_wet * (diag_term[1:-1, 1:-1] * centre + net_x + net_y + net_z)

def reference(start_panel, ocean_mask, conduct_x, conduct_y, conduct_z, diag_shift):
    ocean_cells = ocean_mask.astype(jnp.float32)
    fields = jnp.stack([ocean_cells, conduct_x, conduct_y, conduct_z, diag_shift])
    padded_fields = jnp.pad(fields, ((0, 0), (1, 1), (1, 1), (0, 0)))

    def operate(block):
        return lax.map(lambda single: stencil(jnp.pad(single, ((1, 1), (1, 1), (0, 0))), padded_fields), block)
    field = start_panel * ocean_cells[None]
    for repeat in range(FILTER_STEPS):
        middle = (operate(field) - FILTER_CENTRE * field) / FILTER_HALF
        field = (2.0 * (operate(middle) - FILTER_CENTRE * middle) / FILTER_HALF - field) / FILTER_NORM
    cell_total = NX * NY * NZ
    flattened = field.reshape(PANEL, -1)
    gram_sum = jnp.einsum('kc,lc->kl', flattened, flattened, precision=lax.Precision.HIGHEST) / cell_total
    factor = jnp.linalg.cholesky(gram_sum)
    inverse = lax.linalg.triangular_solve(factor, jnp.eye(PANEL, dtype=jnp.float32), left_side=True, lower=True)
    basis_rows = jnp.einsum('kl,lc->kc', inverse, flattened, precision=lax.Precision.HIGHEST)
    images = operate(basis_rows.reshape(field.shape)).reshape(PANEL, -1)
    projected = jnp.einsum('kc,lc->kl', basis_rows, images, precision=lax.Precision.HIGHEST) / cell_total
    residual = images - jnp.einsum('kl,lc->kc', projected, basis_rows, precision=lax.Precision.HIGHEST)
    return (basis_rows.reshape(field.shape), residual.reshape(field.shape))
```

```python
import jax
import jax.numpy as jnp
from jax import lax
from jax.sharding import PartitionSpec as P

FILTER_STEPS = 2


FILTER_CENTRE = 22.0
FILTER_HALF = 18.0
FILTER_NORM = 2.0 * (22.0 / 18.0) * (22.0 / 18.0) - 1.0

APPLICATIONS = 2 * FILTER_STEPS + 1


def padded_2(block, sides, width):
    for axis, dim in sides:
        count = lax.axis_size(axis)
        forward = [(i, i + 1) for i in range(count - 1)]
        backward = [(target, source) for source, target in forward]
        low = lax.ppermute(
            lax.slice_in_dim(block, block.shape[dim] - width, None, axis=dim), axis, forward
        )
        high = lax.ppermute(lax.slice_in_dim(block, 0, width, axis=dim), axis, backward)
        block = jnp.concatenate([low, block, high], axis=dim)
    return block


def stencil(values, fields):
    wet_mask = fields[0]
    along_x = fields[1]
    along_y = fields[2]
    along_z = fields[3]
    diag_term = fields[4]
    inner_wet = wet_mask[1:-1, 1:-1]
    face_x = along_x[:-1, 1:-1] * wet_mask[:-1, 1:-1] * wet_mask[1:, 1:-1]
    flow_x = face_x * (values[..., 1:, 1:-1, :] - values[..., :-1, 1:-1, :])
    face_y = along_y[1:-1, :-1] * wet_mask[1:-1, :-1] * wet_mask[1:-1, 1:]
    flow_y = face_y * (values[..., 1:-1, 1:, :] - values[..., 1:-1, :-1, :])
    centre = values[..., 1:-1, 1:-1, :]
    face_z = along_z[1:-1, 1:-1, :-1] * inner_wet[:, :, :-1] * inner_wet[:, :, 1:]
    flow_z = face_z * (centre[..., 1:] - centre[..., :-1])
    edges = [(0, 0)] * (centre.ndim - 1)
    net_z = jnp.pad(flow_z, edges + [(1, 0)]) - jnp.pad(flow_z, edges + [(0, 1)])
    net_x = flow_x[..., :-1, :, :] - flow_x[..., 1:, :, :]
    net_y = flow_y[..., :-1, :] - flow_y[..., 1:, :]
    return inner_wet * (diag_term[1:-1, 1:-1] * centre + net_x + net_y + net_z)


def shrink(block, cut, first):
    if cut == 0:
        return block
    block = lax.slice_in_dim(block, cut, block.shape[first] - cut, axis=first)
    return lax.slice_in_dim(block, cut, block.shape[first + 1] - cut, axis=first + 1)


def reduce_all(value):
    for axis in ("gy", "gx"):
        count = lax.axis_size(axis)
        assert count & (count - 1) == 0
        step = 1
        while step < count:
            pairs = [(i, i ^ step) for i in range(count)]
            value = value + lax.ppermute(value, axis, pairs)
            step *= 2
    return value


def inner_products(left, right):
    return jnp.einsum("kc,lc->kl", left, right, precision=lax.Precision.HIGHEST)


def combine(matrix, rows):
    return jnp.einsum("kl,lc->kc", matrix, rows, precision=lax.Precision.HIGHEST)


def triangle_inverse(gram_sum, vectors):
    factor = jnp.linalg.cholesky(gram_sum)
    return lax.linalg.triangular_solve(
        factor, jnp.eye(vectors, dtype=jnp.float32), left_side=True, lower=True
    )


def on_device(start_panel, ocean_mask, conduct_x, conduct_y, conduct_z, diag_shift):
    ocean_cells = ocean_mask.astype(jnp.float32)
    vectors = start_panel.shape[0]
    cell_total = (
        start_panel.shape[1]
        * start_panel.shape[2]
        * start_panel.shape[3]
        * lax.axis_size("gx")
        * lax.axis_size("gy")
    )
    assert APPLICATIONS <= min(start_panel.shape[1], start_panel.shape[2])
    together = jnp.concatenate(
        [
            start_panel * ocean_cells[None],
            jnp.stack([ocean_cells, conduct_x, conduct_y, conduct_z, diag_shift]),
        ]
    )
    together = padded_2(together, (("gx", 1), ("gy", 2)), APPLICATIONS)
    field = together[:vectors]
    fields_all = together[vectors:]
    reach = APPLICATIONS

    def operate(values):
        nonlocal reach
        fields_here = shrink(fields_all, APPLICATIONS - reach, 1)
        reach -= 1
        return stencil(values, fields_here)

    for repeat in range(FILTER_STEPS):
        applied = operate(field)
        field = shrink(field, 1, 1)
        middle = (applied - FILTER_CENTRE * field) / FILTER_HALF
        applied = operate(middle)
        middle = shrink(middle, 1, 1)
        field = shrink(field, 1, 1)
        field = (2.0 * (applied - FILTER_CENTRE * middle) / FILTER_HALF - field) / FILTER_NORM
    raw_images = operate(field)
    field = shrink(field, 1, 1)
    flattened = field.reshape(vectors, -1)
    raw_images = raw_images.reshape(vectors, -1)
    sums = reduce_all(
        jnp.stack([inner_products(flattened, flattened), inner_products(flattened, raw_images)])
    )
    gram_sum = sums[0] / cell_total
    mixed_sum = sums[1] / cell_total
    inverse = triangle_inverse(gram_sum, vectors)
    basis_rows = combine(inverse, flattened)
    images = combine(inverse, raw_images)
    projected = jnp.einsum(
        "ka,ab,lb->kl", inverse, mixed_sum, inverse, precision=lax.Precision.HIGHEST
    )
    residual = images - combine(projected, basis_rows)
    return (basis_rows.reshape(field.shape), residual.reshape(field.shape))


def solution(mesh):
    placed = (
        P(None, "gx", "gy", None),
        P("gx", "gy", None),
        P("gx", "gy", None),
        P("gx", "gy", None),
        P("gx", "gy", None),
        P("gx", "gy", None),
    )
    return jax.shard_map(
        on_device,
        mesh=mesh,
        in_specs=placed,
        out_specs=(P(None, "gx", "gy", None), P(None, "gx", "gy", None)),
        check_vma=False,
    )
```

```python
import jax
import jax.numpy as jnp
from jax import lax
from jax.sharding import PartitionSpec as P

FILTER_STEPS = 2


FILTER_CENTRE = 22.0
FILTER_HALF = 18.0
FILTER_NORM = 2.0 * (22.0 / 18.0) * (22.0 / 18.0) - 1.0


def halo_pair(block, axis, dim):
    count = lax.axis_size(axis)
    forward = [(i, i + 1) for i in range(count - 1)]
    backward = [(target, source) for source, target in forward]
    low = lax.ppermute(lax.slice_in_dim(block, block.shape[dim] - 1, None, axis=dim), axis, forward)
    high = lax.ppermute(lax.slice_in_dim(block, 0, 1, axis=dim), axis, backward)
    return low, high


def padded_2(block, sides, width):
    (axis_a, dim_a), (axis_b, dim_b) = sides
    low_a, high_a = halo_pair(block, axis_a, dim_a)
    low_b, high_b = halo_pair(block, axis_b, dim_b)
    block = jnp.concatenate([low_a, block, high_a], axis=dim_a)
    edge = [(0, 0)] * block.ndim
    edge[dim_a] = (1, 1)
    low_b = jnp.pad(low_b, edge)
    high_b = jnp.pad(high_b, edge)
    return jnp.concatenate([low_b, block, high_b], axis=dim_b)


def stencil(values, fields):
    wet_mask = fields[0]
    along_x = fields[1]
    along_y = fields[2]
    along_z = fields[3]
    diag_term = fields[4]
    inner_wet = wet_mask[1:-1, 1:-1]
    face_x = along_x[:-1, 1:-1] * wet_mask[:-1, 1:-1] * wet_mask[1:, 1:-1]
    flow_x = face_x * (values[..., 1:, 1:-1, :] - values[..., :-1, 1:-1, :])
    face_y = along_y[1:-1, :-1] * wet_mask[1:-1, :-1] * wet_mask[1:-1, 1:]
    flow_y = face_y * (values[..., 1:-1, 1:, :] - values[..., 1:-1, :-1, :])
    centre = values[..., 1:-1, 1:-1, :]
    face_z = along_z[1:-1, 1:-1, :-1] * inner_wet[:, :, :-1] * inner_wet[:, :, 1:]
    flow_z = face_z * (centre[..., 1:] - centre[..., :-1])
    edges = [(0, 0)] * (centre.ndim - 1)
    net_z = jnp.pad(flow_z, edges + [(1, 0)]) - jnp.pad(flow_z, edges + [(0, 1)])
    net_x = flow_x[..., :-1, :, :] - flow_x[..., 1:, :, :]
    net_y = flow_y[..., :-1, :] - flow_y[..., 1:, :]
    return inner_wet * (diag_term[1:-1, 1:-1] * centre + net_x + net_y + net_z)


def operate(block, fields_one):
    padded = padded_2(block, (("gx", 1), ("gy", 2)), 1)
    return stencil(padded, fields_one)


def reduce_all(value):
    for axis in ("gy", "gx"):
        count = lax.axis_size(axis)
        assert count & (count - 1) == 0
        step = 1
        while step < count:
            pairs = [(i, i ^ step) for i in range(count)]
            value = value + lax.ppermute(value, axis, pairs)
            step *= 2
    return value


def inner_products(left, right):
    return jnp.einsum("kc,lc->kl", left, right, precision=lax.Precision.HIGHEST)


def combine(matrix, rows):
    return jnp.einsum("kl,lc->kc", matrix, rows, precision=lax.Precision.HIGHEST)


def triangle_inverse(gram_sum, vectors):
    factor = jnp.linalg.cholesky(gram_sum)
    return lax.linalg.triangular_solve(
        factor, jnp.eye(vectors, dtype=jnp.float32), left_side=True, lower=True
    )


def on_device(start_panel, ocean_mask, conduct_x, conduct_y, conduct_z, diag_shift):
    ocean_cells = ocean_mask.astype(jnp.float32)
    fields = jnp.stack([ocean_cells, conduct_x, conduct_y, conduct_z, diag_shift])
    vectors = start_panel.shape[0]
    cell_total = (
        start_panel.shape[1]
        * start_panel.shape[2]
        * start_panel.shape[3]
        * lax.axis_size("gx")
        * lax.axis_size("gy")
    )
    field = start_panel * ocean_cells[None]
    fields_one = padded_2(fields, (("gx", 1), ("gy", 2)), 1)
    for repeat in range(FILTER_STEPS):
        middle = (operate(field, fields_one) - FILTER_CENTRE * field) / FILTER_HALF
        field = (
            2.0 * (operate(middle, fields_one) - FILTER_CENTRE * middle) / FILTER_HALF - field
        ) / FILTER_NORM
    flattened = field.reshape(vectors, -1)
    raw_images = operate(field, fields_one).reshape(vectors, -1)
    sums = reduce_all(
        jnp.stack([inner_products(flattened, flattened), inner_products(flattened, raw_images)])
    )
    gram_sum = sums[0] / cell_total
    mixed_sum = sums[1] / cell_total
    inverse = triangle_inverse(gram_sum, vectors)
    basis_rows = combine(inverse, flattened)
    images = combine(inverse, raw_images)
    projected = jnp.einsum(
        "ka,ab,lb->kl", inverse, mixed_sum, inverse, precision=lax.Precision.HIGHEST
    )
    residual = images - combine(projected, basis_rows)
    return (basis_rows.reshape(field.shape), residual.reshape(field.shape))


def solution(mesh):
    placed = (
        P(None, "gx", "gy", None),
        P("gx", "gy", None),
        P("gx", "gy", None),
        P("gx", "gy", None),
        P("gx", "gy", None),
        P("gx", "gy", None),
    )
    return jax.shard_map(
        on_device,
        mesh=mesh,
        in_specs=placed,
        out_specs=(P(None, "gx", "gy", None), P(None, "gx", "gy", None)),
        check_vma=False,
    )
```

```python
import jax
import jax.numpy as jnp
from jax import lax
from jax.sharding import PartitionSpec as P

FILTER_STEPS = 2


FILTER_CENTRE = 22.0
FILTER_HALF = 18.0
FILTER_NORM = 2.0 * (22.0 / 18.0) * (22.0 / 18.0) - 1.0


def halo_pair(block, axis, dim):
    count = lax.axis_size(axis)
    forward = [(i, i + 1) for i in range(count - 1)]
    backward = [(target, source) for source, target in forward]
    low = lax.ppermute(lax.slice_in_dim(block, block.shape[dim] - 1, None, axis=dim), axis, forward)
    high = lax.ppermute(lax.slice_in_dim(block, 0, 1, axis=dim), axis, backward)
    return low, high


def padded_2(block, sides, width):
    (axis_a, dim_a), (axis_b, dim_b) = sides
    low_a, high_a = halo_pair(block, axis_a, dim_a)
    low_b, high_b = halo_pair(block, axis_b, dim_b)
    block = jnp.concatenate([low_a, block, high_a], axis=dim_a)
    edge = [(0, 0)] * block.ndim
    edge[dim_a] = (1, 1)
    low_b = jnp.pad(low_b, edge)
    high_b = jnp.pad(high_b, edge)
    return jnp.concatenate([low_b, block, high_b], axis=dim_b)


def stencil(values, fields):
    wet_mask = fields[0]
    along_x = fields[1]
    along_y = fields[2]
    along_z = fields[3]
    diag_term = fields[4]
    inner_wet = wet_mask[1:-1, 1:-1]
    face_x = along_x[:-1, 1:-1] * wet_mask[:-1, 1:-1] * wet_mask[1:, 1:-1]
    flow_x = face_x * (values[..., 1:, 1:-1, :] - values[..., :-1, 1:-1, :])
    face_y = along_y[1:-1, :-1] * wet_mask[1:-1, :-1] * wet_mask[1:-1, 1:]
    flow_y = face_y * (values[..., 1:-1, 1:, :] - values[..., 1:-1, :-1, :])
    centre = values[..., 1:-1, 1:-1, :]
    face_z = along_z[1:-1, 1:-1, :-1] * inner_wet[:, :, :-1] * inner_wet[:, :, 1:]
    flow_z = face_z * (centre[..., 1:] - centre[..., :-1])
    edges = [(0, 0)] * (centre.ndim - 1)
    net_z = jnp.pad(flow_z, edges + [(1, 0)]) - jnp.pad(flow_z, edges + [(0, 1)])
    net_x = flow_x[..., :-1, :, :] - flow_x[..., 1:, :, :]
    net_y = flow_y[..., :-1, :] - flow_y[..., 1:, :]
    return inner_wet * (diag_term[1:-1, 1:-1] * centre + net_x + net_y + net_z)


def operate(block, fields_one):
    padded = padded_2(block, (("gx", 1), ("gy", 2)), 1)
    return stencil(padded, fields_one)


def reduce_all(value):
    for axis in ("gy", "gx"):
        count = lax.axis_size(axis)
        assert count & (count - 1) == 0
        step = 1
        while step < count:
            pairs = [(i, i ^ step) for i in range(count)]
            value = value + lax.ppermute(value, axis, pairs)
            step *= 2
    return value


def inner_products(left, right):
    return jnp.einsum("kc,lc->kl", left, right, precision=lax.Precision.HIGHEST)


def combine(matrix, rows):
    return jnp.einsum("kl,lc->kc", matrix, rows, precision=lax.Precision.HIGHEST)


def triangle_inverse(gram_sum, vectors):
    factor = jnp.linalg.cholesky(gram_sum)
    return lax.linalg.triangular_solve(
        factor, jnp.eye(vectors, dtype=jnp.float32), left_side=True, lower=True
    )


def on_device(start_panel, ocean_mask, conduct_x, conduct_y, conduct_z, diag_shift):
    ocean_cells = ocean_mask.astype(jnp.float32)
    vectors = start_panel.shape[0]
    cell_total = (
        start_panel.shape[1]
        * start_panel.shape[2]
        * start_panel.shape[3]
        * lax.axis_size("gx")
        * lax.axis_size("gy")
    )
    field = start_panel * ocean_cells[None]
    together = padded_2(
        jnp.concatenate(
            [field, jnp.stack([ocean_cells, conduct_x, conduct_y, conduct_z, diag_shift])]
        ),
        (("gx", 1), ("gy", 2)),
        1,
    )
    fields_one = together[vectors:]
    first = True
    for repeat in range(FILTER_STEPS):
        if first:
            applied = stencil(together[:vectors], fields_one)
            first = False
        else:
            applied = operate(field, fields_one)
        middle = (applied - FILTER_CENTRE * field) / FILTER_HALF
        field = (
            2.0 * (operate(middle, fields_one) - FILTER_CENTRE * middle) / FILTER_HALF - field
        ) / FILTER_NORM
    flattened = field.reshape(vectors, -1)
    raw_images = operate(field, fields_one).reshape(vectors, -1)
    sums = reduce_all(
        jnp.stack([inner_products(flattened, flattened), inner_products(flattened, raw_images)])
    )
    gram_sum = sums[0] / cell_total
    mixed_sum = sums[1] / cell_total
    inverse = triangle_inverse(gram_sum, vectors)
    basis_rows = combine(inverse, flattened)
    images = combine(inverse, raw_images)
    projected = jnp.einsum(
        "ka,ab,lb->kl", inverse, mixed_sum, inverse, precision=lax.Precision.HIGHEST
    )
    residual = images - combine(projected, basis_rows)
    return (basis_rows.reshape(field.shape), residual.reshape(field.shape))


def solution(mesh):
    placed = (
        P(None, "gx", "gy", None),
        P("gx", "gy", None),
        P("gx", "gy", None),
        P("gx", "gy", None),
        P("gx", "gy", None),
        P("gx", "gy", None),
    )
    return jax.shard_map(
        on_device,
        mesh=mesh,
        in_specs=placed,
        out_specs=(P(None, "gx", "gy", None), P(None, "gx", "gy", None)),
        check_vma=False,
    )
```

```python
import jax
import jax.numpy as jnp
from jax import lax
from jax.sharding import PartitionSpec as P

FILTER_STEPS = 2
CHUNKS = 2


FILTER_CENTRE = 22.0
FILTER_HALF = 18.0
FILTER_NORM = 2.0 * (22.0 / 18.0) * (22.0 / 18.0) - 1.0


def halo_pair(block, axis, dim):
    count = lax.axis_size(axis)
    forward = [(i, i + 1) for i in range(count - 1)]
    backward = [(target, source) for source, target in forward]
    low = lax.ppermute(lax.slice_in_dim(block, block.shape[dim] - 1, None, axis=dim), axis, forward)
    high = lax.ppermute(lax.slice_in_dim(block, 0, 1, axis=dim), axis, backward)
    return low, high


def padded_2(block, sides, width):
    (axis_a, dim_a), (axis_b, dim_b) = sides
    low_a, high_a = halo_pair(block, axis_a, dim_a)
    low_b, high_b = halo_pair(block, axis_b, dim_b)
    block = jnp.concatenate([low_a, block, high_a], axis=dim_a)
    edge = [(0, 0)] * block.ndim
    edge[dim_a] = (1, 1)
    low_b = jnp.pad(low_b, edge)
    high_b = jnp.pad(high_b, edge)
    return jnp.concatenate([low_b, block, high_b], axis=dim_b)


def stencil(values, fields):
    wet_mask = fields[0]
    along_x = fields[1]
    along_y = fields[2]
    along_z = fields[3]
    diag_term = fields[4]
    inner_wet = wet_mask[1:-1, 1:-1]
    face_x = along_x[:-1, 1:-1] * wet_mask[:-1, 1:-1] * wet_mask[1:, 1:-1]
    flow_x = face_x * (values[..., 1:, 1:-1, :] - values[..., :-1, 1:-1, :])
    face_y = along_y[1:-1, :-1] * wet_mask[1:-1, :-1] * wet_mask[1:-1, 1:]
    flow_y = face_y * (values[..., 1:-1, 1:, :] - values[..., 1:-1, :-1, :])
    centre = values[..., 1:-1, 1:-1, :]
    face_z = along_z[1:-1, 1:-1, :-1] * inner_wet[:, :, :-1] * inner_wet[:, :, 1:]
    flow_z = face_z * (centre[..., 1:] - centre[..., :-1])
    edges = [(0, 0)] * (centre.ndim - 1)
    net_z = jnp.pad(flow_z, edges + [(1, 0)]) - jnp.pad(flow_z, edges + [(0, 1)])
    net_x = flow_x[..., :-1, :, :] - flow_x[..., 1:, :, :]
    net_y = flow_y[..., :-1, :] - flow_y[..., 1:, :]
    return inner_wet * (diag_term[1:-1, 1:-1] * centre + net_x + net_y + net_z)


def operate(block, fields_one):
    padded = padded_2(block, (("gx", 1), ("gy", 2)), 1)
    return stencil(padded, fields_one)


def reduce_all(value):
    for axis in ("gy", "gx"):
        count = lax.axis_size(axis)
        assert count & (count - 1) == 0
        step = 1
        while step < count:
            pairs = [(i, i ^ step) for i in range(count)]
            value = value + lax.ppermute(value, axis, pairs)
            step *= 2
    return value


def inner_products(left, right):
    return jnp.einsum("kc,lc->kl", left, right, precision=lax.Precision.HIGHEST)


def combine(matrix, rows):
    return jnp.einsum("kl,lc->kc", matrix, rows, precision=lax.Precision.HIGHEST)


def triangle_inverse(gram_sum, vectors):
    factor = jnp.linalg.cholesky(gram_sum)
    return lax.linalg.triangular_solve(
        factor, jnp.eye(vectors, dtype=jnp.float32), left_side=True, lower=True
    )


def on_device(start_panel, ocean_mask, conduct_x, conduct_y, conduct_z, diag_shift):
    ocean_cells = ocean_mask.astype(jnp.float32)
    vectors = start_panel.shape[0]
    cell_total = (
        start_panel.shape[1]
        * start_panel.shape[2]
        * start_panel.shape[3]
        * lax.axis_size("gx")
        * lax.axis_size("gy")
    )
    start_field = start_panel * ocean_cells[None]
    share = vectors // CHUNKS
    fields_one = None
    fields_done = []
    images_done = []
    for chunk in range(CHUNKS):
        field = start_field[chunk * share : (chunk + 1) * share]
        if fields_one is None:
            together = padded_2(
                jnp.concatenate(
                    [field, jnp.stack([ocean_cells, conduct_x, conduct_y, conduct_z, diag_shift])]
                ),
                (("gx", 1), ("gy", 2)),
                1,
            )
            fields_one = together[share:]
            applied = stencil(together[:share], fields_one)
        else:
            applied = operate(field, fields_one)
        for repeat in range(FILTER_STEPS):
            if repeat:
                applied = operate(field, fields_one)
            middle = (applied - FILTER_CENTRE * field) / FILTER_HALF
            field = (
                2.0 * (operate(middle, fields_one) - FILTER_CENTRE * middle) / FILTER_HALF - field
            ) / FILTER_NORM
        fields_done.append(field)
        images_done.append(operate(field, fields_one))
    field = jnp.concatenate(fields_done)
    raw_images = jnp.concatenate(images_done).reshape(vectors, -1)
    flattened = field.reshape(vectors, -1)
    raw_images = operate(field, fields_one).reshape(vectors, -1)
    sums = reduce_all(
        jnp.stack([inner_products(flattened, flattened), inner_products(flattened, raw_images)])
    )
    gram_sum = sums[0] / cell_total
    mixed_sum = sums[1] / cell_total
    inverse = triangle_inverse(gram_sum, vectors)
    basis_rows = combine(inverse, flattened)
    images = combine(inverse, raw_images)
    projected = jnp.einsum(
        "ka,ab,lb->kl", inverse, mixed_sum, inverse, precision=lax.Precision.HIGHEST
    )
    residual = images - combine(projected, basis_rows)
    return (basis_rows.reshape(field.shape), residual.reshape(field.shape))


def solution(mesh):
    placed = (
        P(None, "gx", "gy", None),
        P("gx", "gy", None),
        P("gx", "gy", None),
        P("gx", "gy", None),
        P("gx", "gy", None),
        P("gx", "gy", None),
    )
    return jax.shard_map(
        on_device,
        mesh=mesh,
        in_specs=placed,
        out_specs=(P(None, "gx", "gy", None), P(None, "gx", "gy", None)),
        check_vma=False,
    )
```

```python
import functools

import jax
import jax.numpy as jnp
from jax import lax
from jax.experimental import pallas as pl
from jax.experimental.pallas import tpu as pltpu
from jax.sharding import PartitionSpec as P

FILTER_STEPS = 2


FILTER_CENTRE = 22.0
FILTER_HALF = 18.0
FILTER_NORM = 2.0 * (22.0 / 18.0) * (22.0 / 18.0) - 1.0

APPLICATIONS = 2 * FILTER_STEPS + 1
COLUMN_TILE = 8


def padded_deep(block, width, low_pad, total_cols):
    for axis, dim in (("gx", 1), ("gy", 2)):
        count = lax.axis_size(axis)
        forward = [(i, i + 1) for i in range(count - 1)]
        backward = [(target, source) for source, target in forward]
        low = lax.ppermute(
            lax.slice_in_dim(block, block.shape[dim] - width, None, axis=dim), axis, forward
        )
        high = lax.ppermute(lax.slice_in_dim(block, 0, width, axis=dim), axis, backward)
        pieces = [low, block, high]
        if dim == 2:
            shape = list(block.shape)
            shape[2] = low_pad - width
            pieces.insert(0, jnp.zeros(shape, block.dtype))
            shape[2] = total_cols - low_pad - block.shape[2] - width
            pieces.append(jnp.zeros(shape, block.dtype))
        block = jnp.concatenate(pieces, axis=dim)
    return block


def chain_kernel(pan_ref, fld_ref, field_out, raw_out, faces, cur, mid, *, cols, low_pad):
    lanes = fld_ref.shape[-1]
    padded_rows = fld_ref.shape[1]
    padded_cols = fld_ref.shape[2]

    @pl.when(pl.program_id(0) == 0)
    def _():
        lane = lax.broadcasted_iota(jnp.int32, (padded_cols, lanes), 1)

        def face_row(r, carry):
            wet = fld_ref[0, r]
            wet_next = fld_ref[0, jnp.minimum(r + 1, padded_rows - 1)]
            keep = (r + 1 < padded_rows).astype(jnp.float32)
            faces[0, r] = fld_ref[1, r] * wet * (wet_next * keep)
            faces[1, r] = fld_ref[2, r] * wet * pltpu.roll(wet, padded_cols - 1, 0)
            along_z = fld_ref[3, r] * wet * pltpu.roll(wet, lanes - 1, 1)
            faces[2, r] = jnp.where(lane < lanes - 1, along_z, 0.0)
            faces[3, r] = wet * fld_ref[4, r]
            return carry

        lax.fori_loop(0, padded_rows, face_row, 0)

    def apply(src, r):
        centre = src[r]
        flow_hi = faces[0, r] * (src[r + 1] - centre)
        flow_lo = faces[0, r - 1] * (centre - src[r - 1])
        net_x = flow_lo - flow_hi
        flow_y = faces[1, r] * (pltpu.roll(centre, padded_cols - 1, 0) - centre)
        net_y = pltpu.roll(flow_y, 1, 0) - flow_y
        flow_z = faces[2, r] * (pltpu.roll(centre, lanes - 1, 1) - centre)
        net_z = pltpu.roll(flow_z, 1, 1) - flow_z
        return faces[3, r] * centre + net_x + net_y + net_z

    cur[...] = pan_ref[0]

    def first(r, carry):
        mid[r] = (apply(cur, r) - FILTER_CENTRE * cur[r]) * (1.0 / FILTER_HALF)
        return carry

    def second(r, carry):
        cur[r] = (
            2.0 * (apply(mid, r) - FILTER_CENTRE * mid[r]) * (1.0 / FILTER_HALF) - cur[r]
        ) * (1.0 / FILTER_NORM)
        return carry

    reach = 1
    for repeat in range(FILTER_STEPS):
        lax.fori_loop(reach, padded_rows - reach, first, 0, unroll=True)
        reach += 1
        lax.fori_loop(reach, padded_rows - reach, second, 0, unroll=True)
        reach += 1

    def last(r, carry):
        raw_out[0, r - reach] = apply(cur, r)[low_pad : low_pad + cols]
        field_out[0, r - reach] = cur[r][low_pad : low_pad + cols]
        return carry

    lax.fori_loop(reach, padded_rows - reach, last, 0, unroll=True)


def stencil_chain(pan, fld, rows, cols, low_pad):
    vectors, padded_rows, padded_cols, lanes = pan.shape
    kernel = functools.partial(chain_kernel, cols=cols, low_pad=low_pad)
    out = jax.ShapeDtypeStruct((vectors, rows, cols, lanes), jnp.float32)
    return pl.pallas_call(
        kernel,
        grid=(vectors,),
        in_specs=[
            pl.BlockSpec((1, padded_rows, padded_cols, lanes), lambda v: (v, 0, 0, 0)),
            pl.BlockSpec(fld.shape, lambda v: (0, 0, 0, 0)),
        ],
        out_specs=[
            pl.BlockSpec((1, rows, cols, lanes), lambda v: (v, 0, 0, 0)),
            pl.BlockSpec((1, rows, cols, lanes), lambda v: (v, 0, 0, 0)),
        ],
        out_shape=[out, out],
        scratch_shapes=[
            pltpu.VMEM((4, padded_rows, padded_cols, lanes), jnp.float32),
            pltpu.VMEM((padded_rows, padded_cols, lanes), jnp.float32),
            pltpu.VMEM((padded_rows, padded_cols, lanes), jnp.float32),
        ],
    )(pan, fld)


def reduce_all(value):
    for axis in ("gy", "gx"):
        count = lax.axis_size(axis)
        assert count & (count - 1) == 0
        step = 1
        while step < count:
            pairs = [(i, i ^ step) for i in range(count)]
            value = value + lax.ppermute(value, axis, pairs)
            step *= 2
    return value


def inner_products(left, right):
    return jnp.einsum("kc,lc->kl", left, right, precision=lax.Precision.HIGHEST)


def combine(matrix, rows):
    return jnp.einsum("kl,lc->kc", matrix, rows, precision=lax.Precision.HIGHEST)


def triangle_inverse(gram_sum, vectors):
    factor = jnp.linalg.cholesky(gram_sum)
    return lax.linalg.triangular_solve(
        factor, jnp.eye(vectors, dtype=jnp.float32), left_side=True, lower=True
    )


def on_device(start_panel, ocean_mask, conduct_x, conduct_y, conduct_z, diag_shift):
    ocean_cells = ocean_mask.astype(jnp.float32)
    vectors, rows, cols, lanes = start_panel.shape
    cell_total = rows * cols * lanes * lax.axis_size("gx") * lax.axis_size("gy")
    assert APPLICATIONS <= min(rows, cols)
    low_pad = -(-APPLICATIONS // COLUMN_TILE) * COLUMN_TILE
    total_cols = -(-(low_pad + cols + APPLICATIONS) // COLUMN_TILE) * COLUMN_TILE
    together = jnp.concatenate(
        [
            start_panel * ocean_cells[None],
            jnp.stack([ocean_cells, conduct_x, conduct_y, conduct_z, diag_shift]),
        ]
    )
    together = padded_deep(together, APPLICATIONS, low_pad, total_cols)
    field, raw_images = stencil_chain(
        together[:vectors], together[vectors:], rows, cols, low_pad
    )
    flattened = field.reshape(vectors, -1)
    raw_images = raw_images.reshape(vectors, -1)
    sums = reduce_all(
        jnp.stack([inner_products(flattened, flattened), inner_products(flattened, raw_images)])
    )
    gram_sum = sums[0] / cell_total
    mixed_sum = sums[1] / cell_total
    inverse = triangle_inverse(gram_sum, vectors)
    basis_rows = combine(inverse, flattened)
    images = combine(inverse, raw_images)
    projected = jnp.einsum(
        "ka,ab,lb->kl", inverse, mixed_sum, inverse, precision=lax.Precision.HIGHEST
    )
    residual = images - combine(projected, basis_rows)
    return (basis_rows.reshape(field.shape), residual.reshape(field.shape))


def solution(mesh):
    placed = (
        P(None, "gx", "gy", None),
        P("gx", "gy", None),
        P("gx", "gy", None),
        P("gx", "gy", None),
        P("gx", "gy", None),
        P("gx", "gy", None),
    )
    return jax.shard_map(
        on_device,
        mesh=mesh,
        in_specs=placed,
        out_specs=(P(None, "gx", "gy", None), P(None, "gx", "gy", None)),
        check_vma=False,
    )
```

```python
import jax
import jax.numpy as jnp
from jax import lax
from jax.sharding import PartitionSpec as P

FILTER_STEPS = 2


FILTER_CENTRE = 22.0
FILTER_HALF = 18.0
FILTER_NORM = 2.0 * (22.0 / 18.0) * (22.0 / 18.0) - 1.0


def halo_pair(block, axis, dim):
    count = lax.axis_size(axis)
    forward = [(i, i + 1) for i in range(count - 1)]
    backward = [(target, source) for source, target in forward]
    low = lax.ppermute(lax.slice_in_dim(block, block.shape[dim] - 1, None, axis=dim), axis, forward)
    high = lax.ppermute(lax.slice_in_dim(block, 0, 1, axis=dim), axis, backward)
    return low, high


def padded_2(block, sides, width):
    (axis_a, dim_a), (axis_b, dim_b) = sides
    low_a, high_a = halo_pair(block, axis_a, dim_a)
    low_b, high_b = halo_pair(block, axis_b, dim_b)
    block = jnp.concatenate([low_a, block, high_a], axis=dim_a)
    edge = [(0, 0)] * block.ndim
    edge[dim_a] = (1, 1)
    low_b = jnp.pad(low_b, edge)
    high_b = jnp.pad(high_b, edge)
    return jnp.concatenate([low_b, block, high_b], axis=dim_b)


def stencil(values, fields):
    wet_mask = fields[0]
    along_x = fields[1]
    along_y = fields[2]
    along_z = fields[3]
    diag_term = fields[4]
    inner_wet = wet_mask[1:-1, 1:-1]
    face_x = along_x[:-1, 1:-1] * wet_mask[:-1, 1:-1] * wet_mask[1:, 1:-1]
    flow_x = face_x * (values[..., 1:, 1:-1, :] - values[..., :-1, 1:-1, :])
    face_y = along_y[1:-1, :-1] * wet_mask[1:-1, :-1] * wet_mask[1:-1, 1:]
    flow_y = face_y * (values[..., 1:-1, 1:, :] - values[..., 1:-1, :-1, :])
    centre = values[..., 1:-1, 1:-1, :]
    face_z = along_z[1:-1, 1:-1, :-1] * inner_wet[:, :, :-1] * inner_wet[:, :, 1:]
    flow_z = face_z * (centre[..., 1:] - centre[..., :-1])
    edges = [(0, 0)] * (centre.ndim - 1)
    net_z = jnp.pad(flow_z, edges + [(1, 0)]) - jnp.pad(flow_z, edges + [(0, 1)])
    net_x = flow_x[..., :-1, :, :] - flow_x[..., 1:, :, :]
    net_y = flow_y[..., :-1, :] - flow_y[..., 1:, :]
    return inner_wet * (diag_term[1:-1, 1:-1] * centre + net_x + net_y + net_z)


def boundary_faces(fields_one):
    wet, along_x, along_y = fields_one[0], fields_one[1], fields_one[2]
    rows = wet.shape[0] - 2
    cols = wet.shape[1] - 2
    return (
        along_x[0:1, 1:-1] * wet[0:1, 1:-1] * wet[1:2, 1:-1],
        along_x[rows : rows + 1, 1:-1] * wet[rows : rows + 1, 1:-1] * wet[rows + 1 :, 1:-1],
        along_y[1:-1, 0:1] * wet[1:-1, 0:1] * wet[1:-1, 1:2],
        along_y[1:-1, cols : cols + 1] * wet[1:-1, cols : cols + 1] * wet[1:-1, cols + 1 :],
    )


def operate(block, fields_one, faces, scale, finish):
    low_x, high_x = halo_pair(block, "gx", 1)
    low_y, high_y = halo_pair(block, "gy", 2)
    zero_halo = jnp.pad(block, ((0, 0), (1, 1), (1, 1), (0, 0)))
    result = finish(stencil(zero_halo, fields_one))
    rows, cols = block.shape[1], block.shape[2]
    face_lx, face_hx, face_ly, face_hy = faces
    result = result.at[:, 0:1].add(-scale * (face_lx * low_x))
    result = result.at[:, rows - 1 : rows].add(-scale * (face_hx * high_x))
    result = result.at[:, :, 0:1].add(-scale * (face_ly * low_y))
    result = result.at[:, :, cols - 1 : cols].add(-scale * (face_hy * high_y))
    return result


def reduce_all(value):
    for axis in ("gy", "gx"):
        count = lax.axis_size(axis)
        assert count & (count - 1) == 0
        step = 1
        while step < count:
            pairs = [(i, i ^ step) for i in range(count)]
            value = value + lax.ppermute(value, axis, pairs)
            step *= 2
    return value


def inner_products(left, right):
    return jnp.einsum("kc,lc->kl", left, right, precision=lax.Precision.HIGHEST)


def combine(matrix, rows):
    return jnp.einsum("kl,lc->kc", matrix, rows, precision=lax.Precision.HIGHEST)


def triangle_inverse(gram_sum, vectors):
    factor = jnp.linalg.cholesky(gram_sum)
    return lax.linalg.triangular_solve(
        factor, jnp.eye(vectors, dtype=jnp.float32), left_side=True, lower=True
    )


def on_device(start_panel, ocean_mask, conduct_x, conduct_y, conduct_z, diag_shift):
    ocean_cells = ocean_mask.astype(jnp.float32)
    vectors = start_panel.shape[0]
    cell_total = (
        start_panel.shape[1]
        * start_panel.shape[2]
        * start_panel.shape[3]
        * lax.axis_size("gx")
        * lax.axis_size("gy")
    )
    field = start_panel * ocean_cells[None]
    together = padded_2(
        jnp.concatenate(
            [field, jnp.stack([ocean_cells, conduct_x, conduct_y, conduct_z, diag_shift])]
        ),
        (("gx", 1), ("gy", 2)),
        1,
    )
    fields_one = together[vectors:]
    faces = boundary_faces(fields_one)
    for repeat in range(FILTER_STEPS):
        if repeat == 0:
            applied = stencil(together[:vectors], fields_one)
            middle = (applied - FILTER_CENTRE * field) / FILTER_HALF
        else:
            middle = operate(
                field,
                fields_one,
                faces,
                1.0 / FILTER_HALF,
                lambda a, f=field: (a - FILTER_CENTRE * f) / FILTER_HALF,
            )
        field = operate(
            middle,
            fields_one,
            faces,
            2.0 / (FILTER_HALF * FILTER_NORM),
            lambda a, m=middle, f=field: (2.0 * (a - FILTER_CENTRE * m) / FILTER_HALF - f)
            / FILTER_NORM,
        )
    flattened = field.reshape(vectors, -1)
    raw_images = operate(field, fields_one, faces, 1.0, lambda a: a).reshape(vectors, -1)
    sums = reduce_all(
        jnp.stack([inner_products(flattened, flattened), inner_products(flattened, raw_images)])
    )
    gram_sum = sums[0] / cell_total
    mixed_sum = sums[1] / cell_total
    inverse = triangle_inverse(gram_sum, vectors)
    basis_rows = combine(inverse, flattened)
    images = combine(inverse, raw_images)
    projected = jnp.einsum(
        "ka,ab,lb->kl", inverse, mixed_sum, inverse, precision=lax.Precision.HIGHEST
    )
    residual = images - combine(projected, basis_rows)
    return (basis_rows.reshape(field.shape), residual.reshape(field.shape))


def solution(mesh):
    placed = (
        P(None, "gx", "gy", None),
        P("gx", "gy", None),
        P("gx", "gy", None),
        P("gx", "gy", None),
        P("gx", "gy", None),
        P("gx", "gy", None),
    )
    return jax.shard_map(
        on_device,
        mesh=mesh,
        in_specs=placed,
        out_specs=(P(None, "gx", "gy", None), P(None, "gx", "gy", None)),
        check_vma=False,
    )
```

```python
import jax
import jax.numpy as jnp
from jax import lax
from jax.sharding import PartitionSpec as P

FILTER_STEPS = 2


FILTER_CENTRE = 22.0
FILTER_HALF = 18.0
FILTER_NORM = 2.0 * (22.0 / 18.0) * (22.0 / 18.0) - 1.0


def halo_pair(block, axis, dim):
    count = lax.axis_size(axis)
    forward = [(i, i + 1) for i in range(count - 1)]
    backward = [(target, source) for source, target in forward]
    low = lax.ppermute(lax.slice_in_dim(block, block.shape[dim] - 1, None, axis=dim), axis, forward)
    high = lax.ppermute(lax.slice_in_dim(block, 0, 1, axis=dim), axis, backward)
    return low, high


def padded_2(block, sides, width):
    (axis_a, dim_a), (axis_b, dim_b) = sides
    low_a, high_a = halo_pair(block, axis_a, dim_a)
    low_b, high_b = halo_pair(block, axis_b, dim_b)
    block = jnp.concatenate([low_a, block, high_a], axis=dim_a)
    edge = [(0, 0)] * block.ndim
    edge[dim_a] = (1, 1)
    low_b = jnp.pad(low_b, edge)
    high_b = jnp.pad(high_b, edge)
    return jnp.concatenate([low_b, block, high_b], axis=dim_b)


def stencil(values, fields):
    wet_mask = fields[0]
    along_x = fields[1]
    along_y = fields[2]
    along_z = fields[3]
    diag_term = fields[4]
    inner_wet = wet_mask[1:-1, 1:-1]
    face_x = along_x[:-1, 1:-1] * wet_mask[:-1, 1:-1] * wet_mask[1:, 1:-1]
    flow_x = face_x * (values[..., 1:, 1:-1, :] - values[..., :-1, 1:-1, :])
    face_y = along_y[1:-1, :-1] * wet_mask[1:-1, :-1] * wet_mask[1:-1, 1:]
    flow_y = face_y * (values[..., 1:-1, 1:, :] - values[..., 1:-1, :-1, :])
    centre = values[..., 1:-1, 1:-1, :]
    face_z = along_z[1:-1, 1:-1, :-1] * inner_wet[:, :, :-1] * inner_wet[:, :, 1:]
    flow_z = face_z * (centre[..., 1:] - centre[..., :-1])
    edges = [(0, 0)] * (centre.ndim - 1)
    net_z = jnp.pad(flow_z, edges + [(1, 0)]) - jnp.pad(flow_z, edges + [(0, 1)])
    net_x = flow_x[..., :-1, :, :] - flow_x[..., 1:, :, :]
    net_y = flow_y[..., :-1, :] - flow_y[..., 1:, :]
    return inner_wet * (diag_term[1:-1, 1:-1] * centre + net_x + net_y + net_z)


def operate(block, fields_one):
    padded = padded_2(block, (("gx", 1), ("gy", 2)), 1)
    return stencil(padded, fields_one)


def reduce_all(value):
    for axis in ("gy", "gx"):
        count = lax.axis_size(axis)
        assert count & (count - 1) == 0
        step = 1
        while step < count:
            pairs = [(i, i ^ step) for i in range(count)]
            value = value + lax.ppermute(value, axis, pairs)
            step *= 2
    return value


def inner_products(left, right):
    return jnp.einsum("kc,lc->kl", left, right, precision=lax.Precision.HIGHEST)


def combine(matrix, rows):
    return jnp.einsum("kl,lc->kc", matrix, rows, precision=lax.Precision.HIGHEST)


def triangle_inverse(gram_sum, vectors):
    factor = jnp.linalg.cholesky(gram_sum)
    return lax.linalg.triangular_solve(
        factor, jnp.eye(vectors, dtype=jnp.float32), left_side=True, lower=True
    )


def on_device(start_panel, ocean_mask, conduct_x, conduct_y, conduct_z, diag_shift):
    ocean_cells = ocean_mask.astype(jnp.float32)
    vectors = start_panel.shape[0]
    cell_total = (
        start_panel.shape[1]
        * start_panel.shape[2]
        * start_panel.shape[3]
        * lax.axis_size("gx")
        * lax.axis_size("gy")
    )
    field = start_panel * ocean_cells[None]
    together = padded_2(
        jnp.concatenate(
            [field, jnp.stack([ocean_cells, conduct_x, conduct_y, conduct_z, diag_shift])]
        ),
        (("gx", 1), ("gy", 2)),
        1,
    )
    fields_one = together[vectors:]
    first = True
    for repeat in range(FILTER_STEPS):
        if first:
            applied = stencil(together[:vectors], fields_one)
            first = False
        else:
            applied = operate(field, fields_one)
        middle = (applied - FILTER_CENTRE * field) / FILTER_HALF
        field = (
            2.0 * (operate(middle, fields_one) - FILTER_CENTRE * middle) / FILTER_HALF - field
        ) / FILTER_NORM
    flattened = field.reshape(vectors, -1)
    gram_sum = reduce_all(inner_products(flattened, flattened)) / cell_total
    inverse = triangle_inverse(gram_sum, vectors)
    basis_rows = combine(inverse, flattened)
    raw_images = operate(field, fields_one).reshape(vectors, -1)
    mixed_sum = reduce_all(inner_products(flattened, raw_images)) / cell_total
    projected = jnp.einsum(
        "ka,ab,lb->kl", inverse, mixed_sum, inverse, precision=lax.Precision.HIGHEST
    )
    residual = combine(inverse, raw_images) - combine(projected, basis_rows)
    return (basis_rows.reshape(field.shape), residual.reshape(field.shape))


def solution(mesh):
    placed = (
        P(None, "gx", "gy", None),
        P("gx", "gy", None),
        P("gx", "gy", None),
        P("gx", "gy", None),
        P("gx", "gy", None),
        P("gx", "gy", None),
    )
    return jax.shard_map(
        on_device,
        mesh=mesh,
        in_specs=placed,
        out_specs=(P(None, "gx", "gy", None), P(None, "gx", "gy", None)),
        check_vma=False,
    )
```

```python
import jax
import jax.numpy as jnp
from jax import lax
from jax.sharding import PartitionSpec as P

FILTER_STEPS = 2


FILTER_CENTRE = 22.0
FILTER_HALF = 18.0
FILTER_NORM = 2.0 * (22.0 / 18.0) * (22.0 / 18.0) - 1.0


def halo_pair(block, axis, dim):
    count = lax.axis_size(axis)
    forward = [(i, i + 1) for i in range(count - 1)]
    backward = [(target, source) for source, target in forward]
    low = lax.ppermute(lax.slice_in_dim(block, block.shape[dim] - 1, None, axis=dim), axis, forward)
    high = lax.ppermute(lax.slice_in_dim(block, 0, 1, axis=dim), axis, backward)
    return low, high


def padded_2(block, sides, width):
    (axis_a, dim_a), (axis_b, dim_b) = sides
    low_a, high_a = halo_pair(block, axis_a, dim_a)
    low_b, high_b = halo_pair(block, axis_b, dim_b)
    block = jnp.concatenate([low_a, block, high_a], axis=dim_a)
    edge = [(0, 0)] * block.ndim
    edge[dim_a] = (1, 1)
    low_b = jnp.pad(low_b, edge)
    high_b = jnp.pad(high_b, edge)
    return jnp.concatenate([low_b, block, high_b], axis=dim_b)


def stencil(values, fields):
    wet_mask = fields[0]
    along_x = fields[1]
    along_y = fields[2]
    along_z = fields[3]
    diag_term = fields[4]
    inner_wet = wet_mask[1:-1, 1:-1]
    face_x = along_x[:-1, 1:-1] * wet_mask[:-1, 1:-1] * wet_mask[1:, 1:-1]
    flow_x = face_x * (values[..., 1:, 1:-1, :] - values[..., :-1, 1:-1, :])
    face_y = along_y[1:-1, :-1] * wet_mask[1:-1, :-1] * wet_mask[1:-1, 1:]
    flow_y = face_y * (values[..., 1:-1, 1:, :] - values[..., 1:-1, :-1, :])
    centre = values[..., 1:-1, 1:-1, :]
    face_z = along_z[1:-1, 1:-1, :-1] * inner_wet[:, :, :-1] * inner_wet[:, :, 1:]
    flow_z = face_z * (centre[..., 1:] - centre[..., :-1])
    edges = [(0, 0)] * (centre.ndim - 1)
    net_z = jnp.pad(flow_z, edges + [(1, 0)]) - jnp.pad(flow_z, edges + [(0, 1)])
    net_x = flow_x[..., :-1, :, :] - flow_x[..., 1:, :, :]
    net_y = flow_y[..., :-1, :] - flow_y[..., 1:, :]
    return inner_wet * (diag_term[1:-1, 1:-1] * centre + net_x + net_y + net_z)


def operate(block, fields_one):
    padded = padded_2(block, (("gx", 1), ("gy", 2)), 1)
    return stencil(padded, fields_one)


def reduce_all(value):
    for axis in ("gy", "gx"):
        count = lax.axis_size(axis)
        assert count & (count - 1) == 0
        step = 1
        while step < count:
            pairs = [(i, i ^ step) for i in range(count)]
            value = value + lax.ppermute(value, axis, pairs)
            step *= 2
    return value


def inner_products(left, right):
    return jnp.einsum("kc,lc->kl", left, right, precision=lax.Precision.HIGHEST)


def combine(matrix, rows):
    return jnp.einsum("kl,lc->kc", matrix, rows, precision=lax.Precision.HIGHEST)


def triangle_inverse(gram_sum, vectors):
    factor = jnp.linalg.cholesky(gram_sum)
    return lax.linalg.triangular_solve(
        factor, jnp.eye(vectors, dtype=jnp.float32), left_side=True, lower=True
    )


EDGES = ("xlo", "xhi", "ylo", "yhi")


def edges_of(full):
    rows, cols = full.shape[1], full.shape[2]
    return {
        "xlo": full[:, 0:1],
        "xhi": full[:, rows - 1 : rows],
        "ylo": full[:, :, 0:1],
        "yhi": full[:, :, cols - 1 : cols],
    }


def exchange(edges, full):
    count_x = lax.axis_size("gx")
    count_y = lax.axis_size("gy")
    ahead_x = [(i, i + 1) for i in range(count_x - 1)]
    ahead_y = [(i, i + 1) for i in range(count_y - 1)]
    low_x = lax.ppermute(edges["xhi"], "gx", ahead_x)
    high_x = lax.ppermute(edges["xlo"], "gx", [(b, a) for a, b in ahead_x])
    low_y = lax.ppermute(edges["yhi"], "gy", ahead_y)
    high_y = lax.ppermute(edges["ylo"], "gy", [(b, a) for a, b in ahead_y])
    block = jnp.concatenate([low_x, full, high_x], axis=1)
    edge = ((0, 0), (1, 1), (0, 0), (0, 0))
    return jnp.concatenate([jnp.pad(low_y, edge), block, jnp.pad(high_y, edge)], axis=2)


def apply_parts(padded, fields_one):
    rows, cols = padded.shape[1] - 2, padded.shape[2] - 2
    spans = {
        "xlo": (0, 1, 0, cols),
        "xhi": (rows - 1, rows, 0, cols),
        "ylo": (0, rows, 0, 1),
        "yhi": (0, rows, cols - 1, cols),
    }
    parts = {"full": stencil(padded, fields_one)}
    for name, (x0, x1, y0, y1) in spans.items():
        parts[name] = stencil(
            padded[:, x0 : x1 + 2, y0 : y1 + 2], fields_one[:, x0 : x1 + 2, y0 : y1 + 2]
        )
    return parts


def on_device(start_panel, ocean_mask, conduct_x, conduct_y, conduct_z, diag_shift):
    ocean_cells = ocean_mask.astype(jnp.float32)
    vectors = start_panel.shape[0]
    cell_total = (
        start_panel.shape[1]
        * start_panel.shape[2]
        * start_panel.shape[3]
        * lax.axis_size("gx")
        * lax.axis_size("gy")
    )
    field = start_panel * ocean_cells[None]
    together = padded_2(
        jnp.concatenate(
            [field, jnp.stack([ocean_cells, conduct_x, conduct_y, conduct_z, diag_shift])]
        ),
        (("gx", 1), ("gy", 2)),
        1,
    )
    fields_one = together[vectors:]
    field = {"full": field, **edges_of(field)}
    padded = together[:vectors]
    for repeat in range(FILTER_STEPS):
        applied = apply_parts(padded, fields_one)
        middle = {
            name: (applied[name] - FILTER_CENTRE * field[name]) / FILTER_HALF for name in applied
        }
        applied = apply_parts(exchange(middle, middle["full"]), fields_one)
        field = {
            name: (2.0 * (applied[name] - FILTER_CENTRE * middle[name]) / FILTER_HALF - field[name])
            / FILTER_NORM
            for name in applied
        }
        padded = exchange(field, field["full"])
    field = field["full"]
    flattened = field.reshape(vectors, -1)
    gram_sum = reduce_all(inner_products(flattened, flattened)) / cell_total
    inverse = triangle_inverse(gram_sum, vectors)
    basis_rows = combine(inverse, flattened)
    raw_images = stencil(padded, fields_one).reshape(vectors, -1)
    mixed_sum = reduce_all(inner_products(flattened, raw_images)) / cell_total
    projected = jnp.einsum(
        "ka,ab,lb->kl", inverse, mixed_sum, inverse, precision=lax.Precision.HIGHEST
    )
    residual = combine(inverse, raw_images) - combine(projected, basis_rows)
    return (basis_rows.reshape(field.shape), residual.reshape(field.shape))


def solution(mesh):
    placed = (
        P(None, "gx", "gy", None),
        P("gx", "gy", None),
        P("gx", "gy", None),
        P("gx", "gy", None),
        P("gx", "gy", None),
        P("gx", "gy", None),
    )
    return jax.shard_map(
        on_device,
        mesh=mesh,
        in_specs=placed,
        out_specs=(P(None, "gx", "gy", None), P(None, "gx", "gy", None)),
        check_vma=False,
    )
```

```python
import jax
import jax.numpy as jnp
from jax import lax
from jax.sharding import PartitionSpec as P

FILTER_STEPS = 2


FILTER_CENTRE = 22.0
FILTER_HALF = 18.0
FILTER_NORM = 2.0 * (22.0 / 18.0) * (22.0 / 18.0) - 1.0


def halo_pair(block, axis, dim):
    count = lax.axis_size(axis)
    forward = [(i, i + 1) for i in range(count - 1)]
    backward = [(target, source) for source, target in forward]
    low = lax.ppermute(lax.slice_in_dim(block, block.shape[dim] - 1, None, axis=dim), axis, forward)
    high = lax.ppermute(lax.slice_in_dim(block, 0, 1, axis=dim), axis, backward)
    return low, high


def padded_2(block, sides, width):
    (axis_a, dim_a), (axis_b, dim_b) = sides
    low_a, high_a = halo_pair(block, axis_a, dim_a)
    low_b, high_b = halo_pair(block, axis_b, dim_b)
    block = jnp.concatenate([low_a, block, high_a], axis=dim_a)
    edge = [(0, 0)] * block.ndim
    edge[dim_a] = (1, 1)
    low_b = jnp.pad(low_b, edge)
    high_b = jnp.pad(high_b, edge)
    return jnp.concatenate([low_b, block, high_b], axis=dim_b)


def stencil(values, fields):
    wet_mask = fields[0]
    along_x = fields[1]
    along_y = fields[2]
    along_z = fields[3]
    diag_term = fields[4]
    inner_wet = wet_mask[1:-1, 1:-1]
    face_x = along_x[:-1, 1:-1] * wet_mask[:-1, 1:-1] * wet_mask[1:, 1:-1]
    flow_x = face_x * (values[..., 1:, 1:-1, :] - values[..., :-1, 1:-1, :])
    face_y = along_y[1:-1, :-1] * wet_mask[1:-1, :-1] * wet_mask[1:-1, 1:]
    flow_y = face_y * (values[..., 1:-1, 1:, :] - values[..., 1:-1, :-1, :])
    centre = values[..., 1:-1, 1:-1, :]
    face_z = along_z[1:-1, 1:-1, :-1] * inner_wet[:, :, :-1] * inner_wet[:, :, 1:]
    flow_z = face_z * (centre[..., 1:] - centre[..., :-1])
    edges = [(0, 0)] * (centre.ndim - 1)
    net_z = jnp.pad(flow_z, edges + [(1, 0)]) - jnp.pad(flow_z, edges + [(0, 1)])
    net_x = flow_x[..., :-1, :, :] - flow_x[..., 1:, :, :]
    net_y = flow_y[..., :-1, :] - flow_y[..., 1:, :]
    return inner_wet * (diag_term[1:-1, 1:-1] * centre + net_x + net_y + net_z)


def operate(block, fields_one):
    padded = padded_2(block, (("gx", 1), ("gy", 2)), 1)
    return stencil(padded, fields_one)


def reduce_all(value):
    for axis in ("gy", "gx"):
        count = lax.axis_size(axis)
        assert count & (count - 1) == 0
        step = 1
        while step < count:
            pairs = [(i, i ^ step) for i in range(count)]
            value = value + lax.ppermute(value, axis, pairs)
            step *= 2
    return value


def inner_products(left, right):
    return jnp.einsum("kc,lc->kl", left, right, precision=lax.Precision.HIGHEST)


def combine(matrix, rows):
    return jnp.einsum("kl,lc->kc", matrix, rows, precision=lax.Precision.HIGHEST)


def triangle_inverse(gram_sum, vectors):
    factor = jnp.linalg.cholesky(gram_sum)
    return lax.linalg.triangular_solve(
        factor, jnp.eye(vectors, dtype=jnp.float32), left_side=True, lower=True
    )


def on_device(start_panel, ocean_mask, conduct_x, conduct_y, conduct_z, diag_shift):
    ocean_cells = ocean_mask.astype(jnp.float32)
    vectors = start_panel.shape[0]
    cell_total = (
        start_panel.shape[1]
        * start_panel.shape[2]
        * start_panel.shape[3]
        * lax.axis_size("gx")
        * lax.axis_size("gy")
    )
    field = start_panel * ocean_cells[None]
    fields = jnp.stack([ocean_cells, conduct_x, conduct_y, conduct_z, diag_shift])
    rows, cols = field.shape[1], field.shape[2]
    edges = [
        jnp.concatenate([part[:, a:b] for part in (field, fields)])
        for a, b in ((rows - 1, rows), (0, 1))
    ] + [
        jnp.concatenate([part[:, :, a:b] for part in (field, fields)])
        for a, b in ((cols - 1, cols), (0, 1))
    ]
    halos = []
    for axis, (to_high, to_low) in (("gx", edges[0:2]), ("gy", edges[2:4])):
        count = lax.axis_size(axis)
        forward = [(i, i + 1) for i in range(count - 1)]
        backward = [(target, source) for source, target in forward]
        halos += [lax.ppermute(to_high, axis, forward), lax.ppermute(to_low, axis, backward)]

    def assemble(block, part):
        low_x, high_x, low_y, high_y = (halo[part] for halo in halos)
        block = jnp.concatenate([low_x, block, high_x], axis=1)
        edge = ((0, 0), (1, 1), (0, 0), (0, 0))
        return jnp.concatenate([jnp.pad(low_y, edge), block, jnp.pad(high_y, edge)], axis=2)

    fields_one = assemble(fields, slice(vectors, None))
    together = assemble(field, slice(0, vectors))
    first = True
    for repeat in range(FILTER_STEPS):
        if first:
            applied = stencil(together, fields_one)
            first = False
        else:
            applied = operate(field, fields_one)
        middle = (applied - FILTER_CENTRE * field) / FILTER_HALF
        field = (
            2.0 * (operate(middle, fields_one) - FILTER_CENTRE * middle) / FILTER_HALF - field
        ) / FILTER_NORM
    flattened = field.reshape(vectors, -1)
    gram_sum = reduce_all(inner_products(flattened, flattened)) / cell_total
    inverse = triangle_inverse(gram_sum, vectors)
    basis_rows = combine(inverse, flattened)
    raw_images = operate(field, fields_one).reshape(vectors, -1)
    mixed_sum = reduce_all(inner_products(flattened, raw_images)) / cell_total
    projected = jnp.einsum(
        "ka,ab,lb->kl", inverse, mixed_sum, inverse, precision=lax.Precision.HIGHEST
    )
    residual = combine(inverse, raw_images) - combine(projected, basis_rows)
    return (basis_rows.reshape(field.shape), residual.reshape(field.shape))


def solution(mesh):
    placed = (
        P(None, "gx", "gy", None),
        P("gx", "gy", None),
        P("gx", "gy", None),
        P("gx", "gy", None),
        P("gx", "gy", None),
        P("gx", "gy", None),
    )
    return jax.shard_map(
        on_device,
        mesh=mesh,
        in_specs=placed,
        out_specs=(P(None, "gx", "gy", None), P(None, "gx", "gy", None)),
        check_vma=False,
    )
```

```python
import jax
import jax.numpy as jnp
from jax import lax
from jax.sharding import PartitionSpec as P

FILTER_STEPS = 2


FILTER_CENTRE = 22.0
FILTER_HALF = 18.0
FILTER_NORM = 2.0 * (22.0 / 18.0) * (22.0 / 18.0) - 1.0


def halo_pair(block, axis, dim):
    count = lax.axis_size(axis)
    forward = [(i, i + 1) for i in range(count - 1)]
    backward = [(target, source) for source, target in forward]
    low = lax.ppermute(lax.slice_in_dim(block, block.shape[dim] - 1, None, axis=dim), axis, forward)
    high = lax.ppermute(lax.slice_in_dim(block, 0, 1, axis=dim), axis, backward)
    return low, high


def padded_2(block, sides, width):
    (axis_a, dim_a), (axis_b, dim_b) = sides
    low_a, high_a = halo_pair(block, axis_a, dim_a)
    low_b, high_b = halo_pair(block, axis_b, dim_b)
    block = jnp.concatenate([low_a, block, high_a], axis=dim_a)
    edge = [(0, 0)] * block.ndim
    edge[dim_a] = (1, 1)
    low_b = jnp.pad(low_b, edge)
    high_b = jnp.pad(high_b, edge)
    return jnp.concatenate([low_b, block, high_b], axis=dim_b)


def stencil(values, fields):
    wet_mask = fields[0]
    along_x = fields[1]
    along_y = fields[2]
    along_z = fields[3]
    diag_term = fields[4]
    inner_wet = wet_mask[1:-1, 1:-1]
    face_x = along_x[:-1, 1:-1] * wet_mask[:-1, 1:-1] * wet_mask[1:, 1:-1]
    flow_x = face_x * (values[..., 1:, 1:-1, :] - values[..., :-1, 1:-1, :])
    face_y = along_y[1:-1, :-1] * wet_mask[1:-1, :-1] * wet_mask[1:-1, 1:]
    flow_y = face_y * (values[..., 1:-1, 1:, :] - values[..., 1:-1, :-1, :])
    centre = values[..., 1:-1, 1:-1, :]
    face_z = along_z[1:-1, 1:-1, :-1] * inner_wet[:, :, :-1] * inner_wet[:, :, 1:]
    flow_z = face_z * (centre[..., 1:] - centre[..., :-1])
    edges = [(0, 0)] * (centre.ndim - 1)
    net_z = jnp.pad(flow_z, edges + [(1, 0)]) - jnp.pad(flow_z, edges + [(0, 1)])
    net_x = flow_x[..., :-1, :, :] - flow_x[..., 1:, :, :]
    net_y = flow_y[..., :-1, :] - flow_y[..., 1:, :]
    return inner_wet * (diag_term[1:-1, 1:-1] * centre + net_x + net_y + net_z)


def operate(block, fields_one):
    padded = padded_2(block, (("gx", 1), ("gy", 2)), 1)
    return stencil(padded, fields_one)


def reduce_all(value):
    for axis in ("gy", "gx"):
        count = lax.axis_size(axis)
        assert count & (count - 1) == 0
        step = 1
        while step < count:
            pairs = [(i, i ^ step) for i in range(count)]
            value = value + lax.ppermute(value, axis, pairs)
            step *= 2
    return value


def inner_products(left, right):
    return jnp.einsum("kc,lc->kl", left, right, precision=lax.Precision.HIGHEST)


def combine(matrix, rows):
    return jnp.einsum("kl,lc->kc", matrix, rows, precision=lax.Precision.HIGHEST)


def triangle_inverse(gram_sum, vectors):
    factor = jnp.linalg.cholesky(gram_sum)
    return lax.linalg.triangular_solve(
        factor, jnp.eye(vectors, dtype=jnp.float32), left_side=True, lower=True
    )


def on_device(start_panel, ocean_mask, conduct_x, conduct_y, conduct_z, diag_shift):
    ocean_cells = ocean_mask.astype(jnp.float32)
    vectors = start_panel.shape[0]
    cell_total = (
        start_panel.shape[1]
        * start_panel.shape[2]
        * start_panel.shape[3]
        * lax.axis_size("gx")
        * lax.axis_size("gy")
    )
    field = start_panel * ocean_cells[None]
    fields = jnp.stack([ocean_cells, conduct_x, conduct_y, conduct_z, diag_shift])
    rows, cols = field.shape[1], field.shape[2]
    inputs = (ocean_cells, conduct_x, conduct_y, conduct_z, diag_shift)

    def edge(dim, first):
        def cut(a, lead):
            return lax.slice_in_dim(a, first, first + 1, axis=dim + lead)

        panel = cut(start_panel, 1) * cut(ocean_cells, 0)[None]
        return jnp.concatenate([panel, jnp.stack([cut(a, 0) for a in inputs])])

    edges = [edge(0, rows - 1), edge(0, 0), edge(1, cols - 1), edge(1, 0)]
    halos = []
    for axis, (to_high, to_low) in (("gx", edges[0:2]), ("gy", edges[2:4])):
        count = lax.axis_size(axis)
        forward = [(i, i + 1) for i in range(count - 1)]
        backward = [(target, source) for source, target in forward]
        halos += [lax.ppermute(to_high, axis, forward), lax.ppermute(to_low, axis, backward)]

    def assemble(block, part):
        low_x, high_x, low_y, high_y = (halo[part] for halo in halos)
        block = jnp.concatenate([low_x, block, high_x], axis=1)
        ring = ((0, 0), (1, 1), (0, 0), (0, 0))
        return jnp.concatenate([jnp.pad(low_y, ring), block, jnp.pad(high_y, ring)], axis=2)

    fields_one = assemble(fields, slice(vectors, None))
    together = assemble(field, slice(0, vectors))
    first = True
    for repeat in range(FILTER_STEPS):
        if first:
            applied = stencil(together, fields_one)
            first = False
        else:
            applied = operate(field, fields_one)
        middle = (applied - FILTER_CENTRE * field) / FILTER_HALF
        field = (
            2.0 * (operate(middle, fields_one) - FILTER_CENTRE * middle) / FILTER_HALF - field
        ) / FILTER_NORM
    flattened = field.reshape(vectors, -1)
    gram_sum = reduce_all(inner_products(flattened, flattened)) / cell_total
    inverse = triangle_inverse(gram_sum, vectors)
    basis_rows = combine(inverse, flattened)
    raw_images = operate(field, fields_one).reshape(vectors, -1)
    mixed_sum = reduce_all(inner_products(flattened, raw_images)) / cell_total
    projected = jnp.einsum(
        "ka,ab,lb->kl", inverse, mixed_sum, inverse, precision=lax.Precision.HIGHEST
    )
    residual = combine(inverse, raw_images) - combine(projected, basis_rows)
    return (basis_rows.reshape(field.shape), residual.reshape(field.shape))


def solution(mesh):
    placed = (
        P(None, "gx", "gy", None),
        P("gx", "gy", None),
        P("gx", "gy", None),
        P("gx", "gy", None),
        P("gx", "gy", None),
        P("gx", "gy", None),
    )
    return jax.shard_map(
        on_device,
        mesh=mesh,
        in_specs=placed,
        out_specs=(P(None, "gx", "gy", None), P(None, "gx", "gy", None)),
        check_vma=False,
    )
```

```python
import jax
import jax.numpy as jnp
from jax import lax
from jax.sharding import PartitionSpec as P

FILTER_STEPS = 2


FILTER_CENTRE = 22.0
FILTER_HALF = 18.0
FILTER_NORM = 2.0 * (22.0 / 18.0) * (22.0 / 18.0) - 1.0


def halo_pair(block, axis, dim):
    count = lax.axis_size(axis)
    forward = [(i, i + 1) for i in range(count - 1)]
    backward = [(target, source) for source, target in forward]
    low = lax.ppermute(lax.slice_in_dim(block, block.shape[dim] - 1, None, axis=dim), axis, forward)
    high = lax.ppermute(lax.slice_in_dim(block, 0, 1, axis=dim), axis, backward)
    return low, high


def padded_2(block, sides, width):
    (axis_a, dim_a), (axis_b, dim_b) = sides
    low_a, high_a = halo_pair(block, axis_a, dim_a)
    low_b, high_b = halo_pair(block, axis_b, dim_b)
    block = jnp.concatenate([low_a, block, high_a], axis=dim_a)
    edge = [(0, 0)] * block.ndim
    edge[dim_a] = (1, 1)
    low_b = jnp.pad(low_b, edge)
    high_b = jnp.pad(high_b, edge)
    return jnp.concatenate([low_b, block, high_b], axis=dim_b)


def stencil(values, fields):
    wet_mask = fields[0]
    along_x = fields[1]
    along_y = fields[2]
    along_z = fields[3]
    diag_term = fields[4]
    inner_wet = wet_mask[1:-1, 1:-1]
    face_x = along_x[:-1, 1:-1] * wet_mask[:-1, 1:-1] * wet_mask[1:, 1:-1]
    flow_x = face_x * (values[..., 1:, 1:-1, :] - values[..., :-1, 1:-1, :])
    face_y = along_y[1:-1, :-1] * wet_mask[1:-1, :-1] * wet_mask[1:-1, 1:]
    flow_y = face_y * (values[..., 1:-1, 1:, :] - values[..., 1:-1, :-1, :])
    centre = values[..., 1:-1, 1:-1, :]
    face_z = along_z[1:-1, 1:-1, :-1] * inner_wet[:, :, :-1] * inner_wet[:, :, 1:]
    flow_z = face_z * (centre[..., 1:] - centre[..., :-1])
    edges = [(0, 0)] * (centre.ndim - 1)
    net_z = jnp.pad(flow_z, edges + [(1, 0)]) - jnp.pad(flow_z, edges + [(0, 1)])
    net_x = flow_x[..., :-1, :, :] - flow_x[..., 1:, :, :]
    net_y = flow_y[..., :-1, :] - flow_y[..., 1:, :]
    return inner_wet * (diag_term[1:-1, 1:-1] * centre + net_x + net_y + net_z)


def operate(block, fields_one):
    padded = padded_2(block, (("gx", 1), ("gy", 2)), 1)
    return stencil(padded, fields_one)


def boundary_faces(fields_one):
    wet, along_x, along_y = fields_one[0], fields_one[1], fields_one[2]
    rows = wet.shape[0] - 2
    cols = wet.shape[1] - 2
    return (
        along_x[0:1, 1:-1] * wet[0:1, 1:-1] * wet[1:2, 1:-1],
        along_x[rows : rows + 1, 1:-1] * wet[rows : rows + 1, 1:-1] * wet[rows + 1 :, 1:-1],
        along_y[1:-1, 0:1] * wet[1:-1, 0:1] * wet[1:-1, 1:2],
        along_y[1:-1, cols : cols + 1] * wet[1:-1, cols : cols + 1] * wet[1:-1, cols + 1 :],
    )


def reduce_all(value):
    for axis in ("gy", "gx"):
        count = lax.axis_size(axis)
        assert count & (count - 1) == 0
        step = 1
        while step < count:
            pairs = [(i, i ^ step) for i in range(count)]
            value = value + lax.ppermute(value, axis, pairs)
            step *= 2
    return value


def inner_products(left, right):
    return jnp.einsum("kc,lc->kl", left, right, precision=lax.Precision.HIGHEST)


def combine(matrix, rows):
    return jnp.einsum("kl,lc->kc", matrix, rows, precision=lax.Precision.HIGHEST)


def triangle_inverse(gram_sum, vectors):
    factor = jnp.linalg.cholesky(gram_sum)
    return lax.linalg.triangular_solve(
        factor, jnp.eye(vectors, dtype=jnp.float32), left_side=True, lower=True
    )


def on_device(start_panel, ocean_mask, conduct_x, conduct_y, conduct_z, diag_shift):
    ocean_cells = ocean_mask.astype(jnp.float32)
    vectors = start_panel.shape[0]
    cell_total = (
        start_panel.shape[1]
        * start_panel.shape[2]
        * start_panel.shape[3]
        * lax.axis_size("gx")
        * lax.axis_size("gy")
    )
    field = start_panel * ocean_cells[None]
    fields = jnp.stack([ocean_cells, conduct_x, conduct_y, conduct_z, diag_shift])
    rows, cols = field.shape[1], field.shape[2]
    edges = [
        jnp.concatenate([part[:, a:b] for part in (field, fields)])
        for a, b in ((rows - 1, rows), (0, 1))
    ] + [
        jnp.concatenate([part[:, :, a:b] for part in (field, fields)])
        for a, b in ((cols - 1, cols), (0, 1))
    ]
    halos = []
    for axis, (to_high, to_low) in (("gx", edges[0:2]), ("gy", edges[2:4])):
        count = lax.axis_size(axis)
        forward = [(i, i + 1) for i in range(count - 1)]
        backward = [(target, source) for source, target in forward]
        halos += [lax.ppermute(to_high, axis, forward), lax.ppermute(to_low, axis, backward)]

    def assemble(block, part):
        low_x, high_x, low_y, high_y = (halo[part] for halo in halos)
        block = jnp.concatenate([low_x, block, high_x], axis=1)
        edge = ((0, 0), (1, 1), (0, 0), (0, 0))
        return jnp.concatenate([jnp.pad(low_y, edge), block, jnp.pad(high_y, edge)], axis=2)

    fields_one = assemble(fields, slice(vectors, None))
    together = assemble(field, slice(0, vectors))
    first = True
    for repeat in range(FILTER_STEPS):
        if first:
            applied = stencil(together, fields_one)
            first = False
        else:
            applied = operate(field, fields_one)
        middle = (applied - FILTER_CENTRE * field) / FILTER_HALF
        field = (
            2.0 * (operate(middle, fields_one) - FILTER_CENTRE * middle) / FILTER_HALF - field
        ) / FILTER_NORM
    flattened = field.reshape(vectors, -1)
    gram_sum = reduce_all(inner_products(flattened, flattened)) / cell_total
    inverse = triangle_inverse(gram_sum, vectors)
    basis_rows = combine(inverse, flattened)
    low_x, high_x = halo_pair(field, "gx", 1)
    low_y, high_y = halo_pair(field, "gy", 2)
    zero_halo = jnp.pad(field, ((0, 0), (1, 1), (1, 1), (0, 0)))
    mixed_local = inner_products(
        flattened, stencil(zero_halo, fields_one).reshape(vectors, -1)
    )
    face_lx, face_hx, face_ly, face_hy = boundary_faces(fields_one)
    for outer, face, halo in (
        (field[:, 0:1], face_lx, low_x),
        (field[:, rows - 1 : rows], face_hx, high_x),
        (field[:, :, 0:1], face_ly, low_y),
        (field[:, :, cols - 1 : cols], face_hy, high_y),
    ):
        mixed_local = mixed_local - inner_products(
            outer.reshape(vectors, -1), (face * halo).reshape(vectors, -1)
        )
    mixed_sum = reduce_all(mixed_local) / cell_total
    block = jnp.concatenate([low_x, field, high_x], axis=1)
    ring = ((0, 0), (1, 1), (0, 0), (0, 0))
    padded = jnp.concatenate([jnp.pad(low_y, ring), block, jnp.pad(high_y, ring)], axis=2)
    raw_images = stencil(padded, fields_one).reshape(vectors, -1)
    projected = jnp.einsum(
        "ka,ab,lb->kl", inverse, mixed_sum, inverse, precision=lax.Precision.HIGHEST
    )
    residual = combine(inverse, raw_images) - combine(projected, basis_rows)
    return (basis_rows.reshape(field.shape), residual.reshape(field.shape))


def solution(mesh):
    placed = (
        P(None, "gx", "gy", None),
        P("gx", "gy", None),
        P("gx", "gy", None),
        P("gx", "gy", None),
        P("gx", "gy", None),
        P("gx", "gy", None),
    )
    return jax.shard_map(
        on_device,
        mesh=mesh,
        in_specs=placed,
        out_specs=(P(None, "gx", "gy", None), P(None, "gx", "gy", None)),
        check_vma=False,
    )
```

```python
import jax
import jax.numpy as jnp
from jax import lax
from jax.sharding import PartitionSpec as P

FILTER_STEPS = 2


FILTER_CENTRE = 22.0
FILTER_HALF = 18.0
FILTER_NORM = 2.0 * (22.0 / 18.0) * (22.0 / 18.0) - 1.0


def halo_pair(block, axis, dim):
    count = lax.axis_size(axis)
    forward = [(i, i + 1) for i in range(count - 1)]
    backward = [(target, source) for source, target in forward]
    low = lax.ppermute(lax.slice_in_dim(block, block.shape[dim] - 1, None, axis=dim), axis, forward)
    high = lax.ppermute(lax.slice_in_dim(block, 0, 1, axis=dim), axis, backward)
    return low, high


def padded_2(block, sides, width):
    (axis_a, dim_a), (axis_b, dim_b) = sides
    low_a, high_a = halo_pair(block, axis_a, dim_a)
    low_b, high_b = halo_pair(block, axis_b, dim_b)
    block = jnp.concatenate([low_a, block, high_a], axis=dim_a)
    edge = [(0, 0)] * block.ndim
    edge[dim_a] = (1, 1)
    low_b = jnp.pad(low_b, edge)
    high_b = jnp.pad(high_b, edge)
    return jnp.concatenate([low_b, block, high_b], axis=dim_b)


def stencil(values, fields):
    wet_mask = fields[0]
    along_x = fields[1]
    along_y = fields[2]
    along_z = fields[3]
    diag_term = fields[4]
    inner_wet = wet_mask[1:-1, 1:-1]
    face_x = along_x[:-1, 1:-1] * wet_mask[:-1, 1:-1] * wet_mask[1:, 1:-1]
    flow_x = face_x * (values[..., 1:, 1:-1, :] - values[..., :-1, 1:-1, :])
    face_y = along_y[1:-1, :-1] * wet_mask[1:-1, :-1] * wet_mask[1:-1, 1:]
    flow_y = face_y * (values[..., 1:-1, 1:, :] - values[..., 1:-1, :-1, :])
    centre = values[..., 1:-1, 1:-1, :]
    face_z = along_z[1:-1, 1:-1, :-1] * inner_wet[:, :, :-1] * inner_wet[:, :, 1:]
    flow_z = face_z * (centre[..., 1:] - centre[..., :-1])
    edges = [(0, 0)] * (centre.ndim - 1)
    net_z = jnp.pad(flow_z, edges + [(1, 0)]) - jnp.pad(flow_z, edges + [(0, 1)])
    net_x = flow_x[..., :-1, :, :] - flow_x[..., 1:, :, :]
    net_y = flow_y[..., :-1, :] - flow_y[..., 1:, :]
    return inner_wet * (diag_term[1:-1, 1:-1] * centre + net_x + net_y + net_z)


def operate(block, fields_one):
    padded = padded_2(block, (("gx", 1), ("gy", 2)), 1)
    return stencil(padded, fields_one)


def reduce_all(value):
    for axis in ("gy", "gx"):
        count = lax.axis_size(axis)
        assert count & (count - 1) == 0
        step = 1
        while step < count:
            pairs = [(i, i ^ step) for i in range(count)]
            value = value + lax.ppermute(value, axis, pairs)
            step *= 2
    return value


def inner_products(left, right):
    return jnp.einsum("kc,lc->kl", left, right, precision=lax.Precision.HIGHEST)


def combine(matrix, rows):
    return jnp.einsum("kl,lc->kc", matrix, rows, precision=lax.Precision.HIGHEST)


def triangle_inverse(gram_sum, vectors):
    factor = jnp.linalg.cholesky(gram_sum)
    return lax.linalg.triangular_solve(
        factor, jnp.eye(vectors, dtype=jnp.float32), left_side=True, lower=True
    )


def on_device(start_panel, ocean_mask, conduct_x, conduct_y, conduct_z, diag_shift):
    ocean_cells = ocean_mask.astype(jnp.float32)
    vectors = start_panel.shape[0]
    cell_total = (
        start_panel.shape[1]
        * start_panel.shape[2]
        * start_panel.shape[3]
        * lax.axis_size("gx")
        * lax.axis_size("gy")
    )
    field = start_panel * ocean_cells[None]
    fields = jnp.stack([ocean_cells, conduct_x, conduct_y, conduct_z, diag_shift])
    rows, cols = field.shape[1], field.shape[2]
    edges = [
        jnp.concatenate([part[:, a:b] for part in (field, fields)])
        for a, b in ((rows - 1, rows), (0, 1))
    ] + [
        jnp.concatenate([part[:, :, a:b] for part in (field, fields)])
        for a, b in ((cols - 1, cols), (0, 1))
    ]
    halos = []
    for axis, (to_high, to_low) in (("gx", edges[0:2]), ("gy", edges[2:4])):
        count = lax.axis_size(axis)
        forward = [(i, i + 1) for i in range(count - 1)]
        backward = [(target, source) for source, target in forward]
        halos += [lax.ppermute(to_high, axis, forward), lax.ppermute(to_low, axis, backward)]

    def assemble(block, part):
        low_x, high_x, low_y, high_y = (halo[part] for halo in halos)
        block = jnp.concatenate([low_x, block, high_x], axis=1)
        edge = ((0, 0), (1, 1), (0, 0), (0, 0))
        return jnp.concatenate([jnp.pad(low_y, edge), block, jnp.pad(high_y, edge)], axis=2)

    fields_one = assemble(fields, slice(vectors, None))
    together = assemble(field, slice(0, vectors))
    first = True
    for repeat in range(FILTER_STEPS):
        if first:
            applied = stencil(together, fields_one)
            first = False
        else:
            applied = operate(field, fields_one)
        middle = (applied - FILTER_CENTRE * field) / FILTER_HALF
        field = (
            2.0 * (operate(middle, fields_one) - FILTER_CENTRE * middle) / FILTER_HALF - field
        ) / FILTER_NORM
    flattened = field.reshape(vectors, -1)
    low_x, high_x = halo_pair(field, "gx", 1)
    low_y, high_y = halo_pair(field, "gy", 2)
    tie = 0.0 * (low_y[0, 0, 0, 0] + high_y[0, 0, 0, 0])
    gram_sum = reduce_all(inner_products(flattened, flattened) + tie) / cell_total
    inverse = triangle_inverse(gram_sum, vectors)
    basis_rows = combine(inverse, flattened)
    block = jnp.concatenate([low_x, field, high_x], axis=1)
    ring = ((0, 0), (1, 1), (0, 0), (0, 0))
    padded = jnp.concatenate([jnp.pad(low_y, ring), block, jnp.pad(high_y, ring)], axis=2)
    raw_images = stencil(padded, fields_one).reshape(vectors, -1)
    mixed_sum = reduce_all(inner_products(flattened, raw_images)) / cell_total
    projected = jnp.einsum(
        "ka,ab,lb->kl", inverse, mixed_sum, inverse, precision=lax.Precision.HIGHEST
    )
    residual = combine(inverse, raw_images) - combine(projected, basis_rows)
    return (basis_rows.reshape(field.shape), residual.reshape(field.shape))


def solution(mesh):
    placed = (
        P(None, "gx", "gy", None),
        P("gx", "gy", None),
        P("gx", "gy", None),
        P("gx", "gy", None),
        P("gx", "gy", None),
        P("gx", "gy", None),
    )
    return jax.shard_map(
        on_device,
        mesh=mesh,
        in_specs=placed,
        out_specs=(P(None, "gx", "gy", None), P(None, "gx", "gy", None)),
        check_vma=False,
    )
```

```python
import jax
import jax.numpy as jnp
from jax import lax
from jax.sharding import PartitionSpec as P

FILTER_STEPS = 2


FILTER_CENTRE = 22.0
FILTER_HALF = 18.0
FILTER_NORM = 2.0 * (22.0 / 18.0) * (22.0 / 18.0) - 1.0


def halo_pair(block, axis, dim):
    count = lax.axis_size(axis)
    forward = [(i, i + 1) for i in range(count - 1)]
    backward = [(target, source) for source, target in forward]
    low = lax.ppermute(lax.slice_in_dim(block, block.shape[dim] - 1, None, axis=dim), axis, forward)
    high = lax.ppermute(lax.slice_in_dim(block, 0, 1, axis=dim), axis, backward)
    return low, high


def padded_2(block, sides, width):
    (axis_a, dim_a), (axis_b, dim_b) = sides
    low_a, high_a = halo_pair(block, axis_a, dim_a)
    low_b, high_b = halo_pair(block, axis_b, dim_b)
    block = jnp.concatenate([low_a, block, high_a], axis=dim_a)
    edge = [(0, 0)] * block.ndim
    edge[dim_a] = (1, 1)
    low_b = jnp.pad(low_b, edge)
    high_b = jnp.pad(high_b, edge)
    return jnp.concatenate([low_b, block, high_b], axis=dim_b)


def stencil(values, fields):
    wet_mask = fields[0]
    along_x = fields[1]
    along_y = fields[2]
    along_z = fields[3]
    diag_term = fields[4]
    inner_wet = wet_mask[1:-1, 1:-1]
    face_x = along_x[:-1, 1:-1] * wet_mask[:-1, 1:-1] * wet_mask[1:, 1:-1]
    flow_x = face_x * (values[..., 1:, 1:-1, :] - values[..., :-1, 1:-1, :])
    face_y = along_y[1:-1, :-1] * wet_mask[1:-1, :-1] * wet_mask[1:-1, 1:]
    flow_y = face_y * (values[..., 1:-1, 1:, :] - values[..., 1:-1, :-1, :])
    centre = values[..., 1:-1, 1:-1, :]
    face_z = along_z[1:-1, 1:-1, :-1] * inner_wet[:, :, :-1] * inner_wet[:, :, 1:]
    flow_z = face_z * (centre[..., 1:] - centre[..., :-1])
    edges = [(0, 0)] * (centre.ndim - 1)
    net_z = jnp.pad(flow_z, edges + [(1, 0)]) - jnp.pad(flow_z, edges + [(0, 1)])
    net_x = flow_x[..., :-1, :, :] - flow_x[..., 1:, :, :]
    net_y = flow_y[..., :-1, :] - flow_y[..., 1:, :]
    return inner_wet * (diag_term[1:-1, 1:-1] * centre + net_x + net_y + net_z)


def operate(block, fields_one):
    padded = padded_2(block, (("gx", 1), ("gy", 2)), 1)
    return stencil(padded, fields_one)


def reduce_all(value):
    for axis in ("gy", "gx"):
        count = lax.axis_size(axis)
        assert count & (count - 1) == 0
        step = 1
        while step < count:
            pairs = [(i, i ^ step) for i in range(count)]
            value = value + lax.ppermute(value, axis, pairs)
            step *= 2
    return value


def inner_products(left, right):
    return jnp.einsum("kxyz,lxyz->kl", left, right, precision=lax.Precision.HIGHEST)


def combine(matrix, rows):
    return jnp.einsum("kl,lxyz->kxyz", matrix, rows, precision=lax.Precision.HIGHEST)


def triangle_inverse(gram_sum, vectors):
    factor = jnp.linalg.cholesky(gram_sum)
    return lax.linalg.triangular_solve(
        factor, jnp.eye(vectors, dtype=jnp.float32), left_side=True, lower=True
    )


def on_device(start_panel, ocean_mask, conduct_x, conduct_y, conduct_z, diag_shift):
    ocean_cells = ocean_mask.astype(jnp.float32)
    vectors = start_panel.shape[0]
    cell_total = (
        start_panel.shape[1]
        * start_panel.shape[2]
        * start_panel.shape[3]
        * lax.axis_size("gx")
        * lax.axis_size("gy")
    )
    field = start_panel * ocean_cells[None]
    fields = jnp.stack([ocean_cells, conduct_x, conduct_y, conduct_z, diag_shift])
    rows, cols = field.shape[1], field.shape[2]
    edges = [
        jnp.concatenate([part[:, a:b] for part in (field, fields)])
        for a, b in ((rows - 1, rows), (0, 1))
    ] + [
        jnp.concatenate([part[:, :, a:b] for part in (field, fields)])
        for a, b in ((cols - 1, cols), (0, 1))
    ]
    halos = []
    for axis, (to_high, to_low) in (("gx", edges[0:2]), ("gy", edges[2:4])):
        count = lax.axis_size(axis)
        forward = [(i, i + 1) for i in range(count - 1)]
        backward = [(target, source) for source, target in forward]
        halos += [lax.ppermute(to_high, axis, forward), lax.ppermute(to_low, axis, backward)]

    def assemble(block, part):
        low_x, high_x, low_y, high_y = (halo[part] for halo in halos)
        block = jnp.concatenate([low_x, block, high_x], axis=1)
        edge = ((0, 0), (1, 1), (0, 0), (0, 0))
        return jnp.concatenate([jnp.pad(low_y, edge), block, jnp.pad(high_y, edge)], axis=2)

    fields_one = assemble(fields, slice(vectors, None))
    together = assemble(field, slice(0, vectors))
    first = True
    for repeat in range(FILTER_STEPS):
        if first:
            applied = stencil(together, fields_one)
            first = False
        else:
            applied = operate(field, fields_one)
        middle = (applied - FILTER_CENTRE * field) / FILTER_HALF
        field = (
            2.0 * (operate(middle, fields_one) - FILTER_CENTRE * middle) / FILTER_HALF - field
        ) / FILTER_NORM
    flattened = field
    gram_sum = reduce_all(inner_products(flattened, flattened)) / cell_total
    inverse = triangle_inverse(gram_sum, vectors)
    basis_rows = combine(inverse, flattened)
    raw_images = operate(field, fields_one)
    mixed_sum = reduce_all(inner_products(flattened, raw_images)) / cell_total
    projected = jnp.einsum(
        "ka,ab,lb->kl", inverse, mixed_sum, inverse, precision=lax.Precision.HIGHEST
    )
    residual = combine(inverse, raw_images) - combine(projected, basis_rows)
    return (basis_rows, residual)


def solution(mesh):
    placed = (
        P(None, "gx", "gy", None),
        P("gx", "gy", None),
        P("gx", "gy", None),
        P("gx", "gy", None),
        P("gx", "gy", None),
        P("gx", "gy", None),
    )
    return jax.shard_map(
        on_device,
        mesh=mesh,
        in_specs=placed,
        out_specs=(P(None, "gx", "gy", None), P(None, "gx", "gy", None)),
        check_vma=False,
    )
```

```python
import jax
import jax.numpy as jnp
from jax import lax
from jax.sharding import PartitionSpec as P

FILTER_STEPS = 2


FILTER_CENTRE = 22.0
FILTER_HALF = 18.0
FILTER_NORM = 2.0 * (22.0 / 18.0) * (22.0 / 18.0) - 1.0


def halo_pair(block, axis, dim):
    count = lax.axis_size(axis)
    forward = [(i, i + 1) for i in range(count - 1)]
    backward = [(target, source) for source, target in forward]
    low = lax.ppermute(lax.slice_in_dim(block, block.shape[dim] - 1, None, axis=dim), axis, forward)
    high = lax.ppermute(lax.slice_in_dim(block, 0, 1, axis=dim), axis, backward)
    return low, high


def padded_2(block, sides, width):
    (axis_a, dim_a), (axis_b, dim_b) = sides
    low_a, high_a = halo_pair(block, axis_a, dim_a)
    low_b, high_b = halo_pair(block, axis_b, dim_b)
    block = jnp.concatenate([low_a, block, high_a], axis=dim_a)
    edge = [(0, 0)] * block.ndim
    edge[dim_a] = (1, 1)
    low_b = jnp.pad(low_b, edge)
    high_b = jnp.pad(high_b, edge)
    return jnp.concatenate([low_b, block, high_b], axis=dim_b)


def stencil(values, fields):
    wet_mask = fields[0]
    along_x = fields[1]
    along_y = fields[2]
    along_z = fields[3]
    diag_term = fields[4]
    inner_wet = wet_mask[1:-1, 1:-1]
    face_x = along_x[:-1, 1:-1] * wet_mask[:-1, 1:-1] * wet_mask[1:, 1:-1]
    flow_x = face_x * (values[..., 1:, 1:-1, :] - values[..., :-1, 1:-1, :])
    face_y = along_y[1:-1, :-1] * wet_mask[1:-1, :-1] * wet_mask[1:-1, 1:]
    flow_y = face_y * (values[..., 1:-1, 1:, :] - values[..., 1:-1, :-1, :])
    centre = values[..., 1:-1, 1:-1, :]
    face_z = along_z[1:-1, 1:-1, :-1] * inner_wet[:, :, :-1] * inner_wet[:, :, 1:]
    flow_z = face_z * (centre[..., 1:] - centre[..., :-1])
    edges = [(0, 0)] * (centre.ndim - 1)
    net_z = jnp.pad(flow_z, edges + [(1, 0)]) - jnp.pad(flow_z, edges + [(0, 1)])
    net_x = flow_x[..., :-1, :, :] - flow_x[..., 1:, :, :]
    net_y = flow_y[..., :-1, :] - flow_y[..., 1:, :]
    return inner_wet * (diag_term[1:-1, 1:-1] * centre + net_x + net_y + net_z)


def operate(block, fields_one):
    padded = padded_2(block, (("gx", 1), ("gy", 2)), 1)
    return stencil(padded, fields_one)


def reduce_all(value):
    for axis in ("gy", "gx"):
        count = lax.axis_size(axis)
        assert count & (count - 1) == 0
        step = 1
        while step < count:
            pairs = [(i, i ^ step) for i in range(count)]
            value = value + lax.ppermute(value, axis, pairs)
            step *= 2
    return value


def inner_products(left, right):
    return jnp.einsum("kc,lc->kl", left, right, precision=lax.Precision.HIGHEST)


def combine(matrix, rows):
    return jnp.einsum("kl,lc->kc", matrix, rows, precision=lax.Precision.HIGHEST)


def triangle_inverse(gram_sum, vectors):
    factor = jnp.linalg.cholesky(gram_sum)
    return lax.linalg.triangular_solve(
        factor, jnp.eye(vectors, dtype=jnp.float32), left_side=True, lower=True
    )


def on_device(start_panel, ocean_mask, conduct_x, conduct_y, conduct_z, diag_shift):
    ocean_cells = ocean_mask.astype(jnp.float32)
    vectors = start_panel.shape[0]
    cell_total = (
        start_panel.shape[1]
        * start_panel.shape[2]
        * start_panel.shape[3]
        * lax.axis_size("gx")
        * lax.axis_size("gy")
    )
    field = start_panel * ocean_cells[None]
    fields = jnp.stack([ocean_cells, conduct_x, conduct_y, conduct_z, diag_shift])
    rows, cols = field.shape[1], field.shape[2]
    sent = ((0, 1), (0,), (0, 2), (0,))
    edges = []
    for (dim, first), keep in zip(
        ((0, rows - 1), (0, 0), (1, cols - 1), (1, 0)), sent
    ):
        cut = lambda a, lead: lax.slice_in_dim(a, first, first + 1, axis=dim + lead)
        edges.append(
            jnp.concatenate([cut(field, 1), *(cut(fields[i : i + 1], 1) for i in keep)])
        )
    halos = []
    for axis, (to_high, to_low) in (("gx", edges[0:2]), ("gy", edges[2:4])):
        count = lax.axis_size(axis)
        forward = [(i, i + 1) for i in range(count - 1)]
        backward = [(target, source) for source, target in forward]
        halos += [lax.ppermute(to_high, axis, forward), lax.ppermute(to_low, axis, backward)]

    def widen(halo, keep):
        parts = [jnp.zeros_like(halo[vectors : vectors + 1])] * fields.shape[0]
        for place, index in enumerate(keep):
            parts[index] = halo[vectors + place : vectors + place + 1]
        return jnp.concatenate(parts)

    def assemble(block, low_x, high_x, low_y, high_y):
        block = jnp.concatenate([low_x, block, high_x], axis=1)
        edge = ((0, 0), (1, 1), (0, 0), (0, 0))
        return jnp.concatenate([jnp.pad(low_y, edge), block, jnp.pad(high_y, edge)], axis=2)

    fields_one = assemble(fields, *(widen(halo, keep) for halo, keep in zip(halos, sent)))
    together = assemble(field, *(halo[:vectors] for halo in halos))
    first = True
    for repeat in range(FILTER_STEPS):
        if first:
            applied = stencil(together, fields_one)
            first = False
        else:
            applied = operate(field, fields_one)
        middle = (applied - FILTER_CENTRE * field) / FILTER_HALF
        field = (
            2.0 * (operate(middle, fields_one) - FILTER_CENTRE * middle) / FILTER_HALF - field
        ) / FILTER_NORM
    flattened = field.reshape(vectors, -1)
    gram_sum = reduce_all(inner_products(flattened, flattened)) / cell_total
    inverse = triangle_inverse(gram_sum, vectors)
    basis_rows = combine(inverse, flattened)
    raw_images = operate(field, fields_one).reshape(vectors, -1)
    mixed_sum = reduce_all(inner_products(flattened, raw_images)) / cell_total
    projected = jnp.einsum(
        "ka,ab,lb->kl", inverse, mixed_sum, inverse, precision=lax.Precision.HIGHEST
    )
    residual = combine(inverse, raw_images) - combine(projected, basis_rows)
    return (basis_rows.reshape(field.shape), residual.reshape(field.shape))


def solution(mesh):
    placed = (
        P(None, "gx", "gy", None),
        P("gx", "gy", None),
        P("gx", "gy", None),
        P("gx", "gy", None),
        P("gx", "gy", None),
        P("gx", "gy", None),
    )
    return jax.shard_map(
        on_device,
        mesh=mesh,
        in_specs=placed,
        out_specs=(P(None, "gx", "gy", None), P(None, "gx", "gy", None)),
        check_vma=False,
    )
```

```python
import jax
import jax.numpy as jnp
from jax import lax
from jax.sharding import PartitionSpec as P

FILTER_STEPS = 2


FILTER_CENTRE = 22.0
FILTER_HALF = 18.0
FILTER_NORM = 2.0 * (22.0 / 18.0) * (22.0 / 18.0) - 1.0


def swap_halos(to_high, to_low, axis):
    count = lax.axis_size(axis)
    even = lax.axis_index(axis) % 2 == 0
    first = [(i, i ^ 1) for i in range(count - count % 2)]
    second = [(i, j) for i in range(1, count - 1) for j in (i + 1 if i % 2 else i - 1,)]
    got_first = lax.ppermute(jnp.where(even, to_high, to_low), axis, first)
    got_second = lax.ppermute(jnp.where(even, to_low, to_high), axis, second)
    low = jnp.where(even, got_second, got_first)
    high = jnp.where(even, got_first, got_second)
    return low, high


def halo_pair(block, axis, dim):
    return swap_halos(
        lax.slice_in_dim(block, block.shape[dim] - 1, None, axis=dim),
        lax.slice_in_dim(block, 0, 1, axis=dim),
        axis,
    )


def padded_2(block, sides, width):
    (axis_a, dim_a), (axis_b, dim_b) = sides
    low_a, high_a = halo_pair(block, axis_a, dim_a)
    low_b, high_b = halo_pair(block, axis_b, dim_b)
    block = jnp.concatenate([low_a, block, high_a], axis=dim_a)
    edge = [(0, 0)] * block.ndim
    edge[dim_a] = (1, 1)
    low_b = jnp.pad(low_b, edge)
    high_b = jnp.pad(high_b, edge)
    return jnp.concatenate([low_b, block, high_b], axis=dim_b)


def stencil(values, fields):
    wet_mask = fields[0]
    along_x = fields[1]
    along_y = fields[2]
    along_z = fields[3]
    diag_term = fields[4]
    inner_wet = wet_mask[1:-1, 1:-1]
    face_x = along_x[:-1, 1:-1] * wet_mask[:-1, 1:-1] * wet_mask[1:, 1:-1]
    flow_x = face_x * (values[..., 1:, 1:-1, :] - values[..., :-1, 1:-1, :])
    face_y = along_y[1:-1, :-1] * wet_mask[1:-1, :-1] * wet_mask[1:-1, 1:]
    flow_y = face_y * (values[..., 1:-1, 1:, :] - values[..., 1:-1, :-1, :])
    centre = values[..., 1:-1, 1:-1, :]
    face_z = along_z[1:-1, 1:-1, :-1] * inner_wet[:, :, :-1] * inner_wet[:, :, 1:]
    flow_z = face_z * (centre[..., 1:] - centre[..., :-1])
    edges = [(0, 0)] * (centre.ndim - 1)
    net_z = jnp.pad(flow_z, edges + [(1, 0)]) - jnp.pad(flow_z, edges + [(0, 1)])
    net_x = flow_x[..., :-1, :, :] - flow_x[..., 1:, :, :]
    net_y = flow_y[..., :-1, :] - flow_y[..., 1:, :]
    return inner_wet * (diag_term[1:-1, 1:-1] * centre + net_x + net_y + net_z)


def operate(block, fields_one):
    padded = padded_2(block, (("gx", 1), ("gy", 2)), 1)
    return stencil(padded, fields_one)


def reduce_all(value):
    for axis in ("gy", "gx"):
        count = lax.axis_size(axis)
        assert count & (count - 1) == 0
        step = 1
        while step < count:
            pairs = [(i, i ^ step) for i in range(count)]
            value = value + lax.ppermute(value, axis, pairs)
            step *= 2
    return value


def inner_products(left, right):
    return jnp.einsum("kc,lc->kl", left, right, precision=lax.Precision.HIGHEST)


def combine(matrix, rows):
    return jnp.einsum("kl,lc->kc", matrix, rows, precision=lax.Precision.HIGHEST)


def triangle_inverse(gram_sum, vectors):
    factor = jnp.linalg.cholesky(gram_sum)
    return lax.linalg.triangular_solve(
        factor, jnp.eye(vectors, dtype=jnp.float32), left_side=True, lower=True
    )


def on_device(start_panel, ocean_mask, conduct_x, conduct_y, conduct_z, diag_shift):
    ocean_cells = ocean_mask.astype(jnp.float32)
    vectors = start_panel.shape[0]
    cell_total = (
        start_panel.shape[1]
        * start_panel.shape[2]
        * start_panel.shape[3]
        * lax.axis_size("gx")
        * lax.axis_size("gy")
    )
    field = start_panel * ocean_cells[None]
    fields = jnp.stack([ocean_cells, conduct_x, conduct_y, conduct_z, diag_shift])
    rows, cols = field.shape[1], field.shape[2]
    sent = ((0, 1), (0,), (0, 2), (0,))
    edges = []
    for (dim, first), keep in zip(
        ((0, rows - 1), (0, 0), (1, cols - 1), (1, 0)), sent
    ):
        cut = lambda a, lead: lax.slice_in_dim(a, first, first + 1, axis=dim + lead)
        edges.append(
            jnp.concatenate([cut(field, 1), *(cut(fields[i : i + 1], 1) for i in keep)])
        )
    halos = []
    for axis, (to_high, to_low), (keep_high, keep_low) in (
        ("gx", edges[0:2], sent[0:2]),
        ("gy", edges[2:4], sent[2:4]),
    ):
        size = max(to_high.shape[0], to_low.shape[0])
        grow = lambda a: jnp.pad(a, ((0, size - a.shape[0]),) + ((0, 0),) * (a.ndim - 1))
        low, high = swap_halos(grow(to_high), grow(to_low), axis)
        halos += [low[: to_high.shape[0]], high[: to_low.shape[0]]]

    def widen(halo, keep):
        parts = [jnp.zeros_like(halo[vectors : vectors + 1])] * fields.shape[0]
        for place, index in enumerate(keep):
            parts[index] = halo[vectors + place : vectors + place + 1]
        return jnp.concatenate(parts)

    def assemble(block, low_x, high_x, low_y, high_y):
        block = jnp.concatenate([low_x, block, high_x], axis=1)
        edge = ((0, 0), (1, 1), (0, 0), (0, 0))
        return jnp.concatenate([jnp.pad(low_y, edge), block, jnp.pad(high_y, edge)], axis=2)

    fields_one = assemble(fields, *(widen(halo, keep) for halo, keep in zip(halos, sent)))
    together = assemble(field, *(halo[:vectors] for halo in halos))
    first = True
    for repeat in range(FILTER_STEPS):
        if first:
            applied = stencil(together, fields_one)
            first = False
        else:
            applied = operate(field, fields_one)
        middle = (applied - FILTER_CENTRE * field) / FILTER_HALF
        field = (
            2.0 * (operate(middle, fields_one) - FILTER_CENTRE * middle) / FILTER_HALF - field
        ) / FILTER_NORM
    flattened = field.reshape(vectors, -1)
    gram_sum = reduce_all(inner_products(flattened, flattened)) / cell_total
    inverse = triangle_inverse(gram_sum, vectors)
    basis_rows = combine(inverse, flattened)
    raw_images = operate(field, fields_one).reshape(vectors, -1)
    mixed_sum = reduce_all(inner_products(flattened, raw_images)) / cell_total
    projected = jnp.einsum(
        "ka,ab,lb->kl", inverse, mixed_sum, inverse, precision=lax.Precision.HIGHEST
    )
    residual = combine(inverse, raw_images) - combine(projected, basis_rows)
    return (basis_rows.reshape(field.shape), residual.reshape(field.shape))


def solution(mesh):
    placed = (
        P(None, "gx", "gy", None),
        P("gx", "gy", None),
        P("gx", "gy", None),
        P("gx", "gy", None),
        P("gx", "gy", None),
        P("gx", "gy", None),
    )
    return jax.shard_map(
        on_device,
        mesh=mesh,
        in_specs=placed,
        out_specs=(P(None, "gx", "gy", None), P(None, "gx", "gy", None)),
        check_vma=False,
    )
```

```python
import jax
import jax.numpy as jnp
from jax import lax
from jax.sharding import PartitionSpec as P

FILTER_STEPS = 2


FILTER_CENTRE = 22.0
FILTER_HALF = 18.0
FILTER_NORM = 2.0 * (22.0 / 18.0) * (22.0 / 18.0) - 1.0


def swap_halos(to_high, to_low, axis):
    count = lax.axis_size(axis)
    even = lax.axis_index(axis) % 2 == 0
    first = [(i, i ^ 1) for i in range(count - count % 2)]
    second = [(i, j) for i in range(1, count - 1) for j in (i + 1 if i % 2 else i - 1,)]
    got_first = lax.ppermute(jnp.where(even, to_high, to_low), axis, first)
    got_second = lax.ppermute(jnp.where(even, to_low, to_high), axis, second)
    low = jnp.where(even, got_second, got_first)
    high = jnp.where(even, got_first, got_second)
    return low, high


def halo_pair(block, axis, dim):
    return swap_halos(
        lax.slice_in_dim(block, block.shape[dim] - 1, None, axis=dim),
        lax.slice_in_dim(block, 0, 1, axis=dim),
        axis,
    )


def padded_2(block, sides, width):
    (axis_a, dim_a), (axis_b, dim_b) = sides
    low_a, high_a = halo_pair(block, axis_a, dim_a)
    low_b, high_b = halo_pair(block, axis_b, dim_b)
    block = jnp.concatenate([low_a, block, high_a], axis=dim_a)
    edge = [(0, 0)] * block.ndim
    edge[dim_a] = (1, 1)
    low_b = jnp.pad(low_b, edge)
    high_b = jnp.pad(high_b, edge)
    return jnp.concatenate([low_b, block, high_b], axis=dim_b)


def stencil(values, fields):
    wet_mask = fields[0]
    along_x = fields[1]
    along_y = fields[2]
    along_z = fields[3]
    diag_term = fields[4]
    inner_wet = wet_mask[1:-1, 1:-1]
    face_x = along_x[:-1, 1:-1] * wet_mask[:-1, 1:-1] * wet_mask[1:, 1:-1]
    flow_x = face_x * (values[..., 1:, 1:-1, :] - values[..., :-1, 1:-1, :])
    face_y = along_y[1:-1, :-1] * wet_mask[1:-1, :-1] * wet_mask[1:-1, 1:]
    flow_y = face_y * (values[..., 1:-1, 1:, :] - values[..., 1:-1, :-1, :])
    centre = values[..., 1:-1, 1:-1, :]
    face_z = along_z[1:-1, 1:-1, :-1] * inner_wet[:, :, :-1] * inner_wet[:, :, 1:]
    flow_z = face_z * (centre[..., 1:] - centre[..., :-1])
    edges = [(0, 0)] * (centre.ndim - 1)
    net_z = jnp.pad(flow_z, edges + [(1, 0)]) - jnp.pad(flow_z, edges + [(0, 1)])
    net_x = flow_x[..., :-1, :, :] - flow_x[..., 1:, :, :]
    net_y = flow_y[..., :-1, :] - flow_y[..., 1:, :]
    return inner_wet * (diag_term[1:-1, 1:-1] * centre + net_x + net_y + net_z)


def operate(block, fields_one):
    low_x, high_x = halo_pair(block, "gx", 1)
    low_y, high_y = halo_pair(block, "gy", 2)
    rows = block.shape[1]
    padded = jnp.concatenate([jnp.zeros_like(low_x), block, jnp.zeros_like(high_x)], axis=1)
    ring = ((0, 0), (1, 1), (0, 0), (0, 0))
    padded = jnp.concatenate([jnp.pad(low_y, ring), padded, jnp.pad(high_y, ring)], axis=2)
    applied = stencil(padded, fields_one)
    wet, along_x = fields_one[0], fields_one[1]
    face_low = along_x[0:1, 1:-1] * wet[0:1, 1:-1] * wet[1:2, 1:-1]
    face_high = along_x[rows : rows + 1, 1:-1] * wet[rows : rows + 1, 1:-1] * wet[rows + 1 :, 1:-1]
    applied = lax.dynamic_update_slice_in_dim(
        applied, applied[:, 0:1] - face_low * low_x, 0, axis=1
    )
    return lax.dynamic_update_slice_in_dim(
        applied, applied[:, rows - 1 : rows] - face_high * high_x, rows - 1, axis=1
    )


def reduce_all(value):
    for axis in ("gy", "gx"):
        count = lax.axis_size(axis)
        assert count & (count - 1) == 0
        step = 1
        while step < count:
            pairs = [(i, i ^ step) for i in range(count)]
            value = value + lax.ppermute(value, axis, pairs)
            step *= 2
    return value


def inner_products(left, right):
    return jnp.einsum("kc,lc->kl", left, right, precision=lax.Precision.HIGHEST)


def combine(matrix, rows):
    return jnp.einsum("kl,lc->kc", matrix, rows, precision=lax.Precision.HIGHEST)


def triangle_inverse(gram_sum, vectors):
    factor = jnp.linalg.cholesky(gram_sum)
    return lax.linalg.triangular_solve(
        factor, jnp.eye(vectors, dtype=jnp.float32), left_side=True, lower=True
    )


def on_device(start_panel, ocean_mask, conduct_x, conduct_y, conduct_z, diag_shift):
    ocean_cells = ocean_mask.astype(jnp.float32)
    vectors = start_panel.shape[0]
    cell_total = (
        start_panel.shape[1]
        * start_panel.shape[2]
        * start_panel.shape[3]
        * lax.axis_size("gx")
        * lax.axis_size("gy")
    )
    field = start_panel * ocean_cells[None]
    fields = jnp.stack([ocean_cells, conduct_x, conduct_y, conduct_z, diag_shift])
    rows, cols = field.shape[1], field.shape[2]
    sent = ((0, 1), (0,), (0, 2), (0,))
    edges = []
    for (dim, first), keep in zip(
        ((0, rows - 1), (0, 0), (1, cols - 1), (1, 0)), sent
    ):
        cut = lambda a, lead: lax.slice_in_dim(a, first, first + 1, axis=dim + lead)
        edges.append(
            jnp.concatenate([cut(field, 1), *(cut(fields[i : i + 1], 1) for i in keep)])
        )
    halos = []
    for axis, (to_high, to_low), (keep_high, keep_low) in (
        ("gx", edges[0:2], sent[0:2]),
        ("gy", edges[2:4], sent[2:4]),
    ):
        size = max(to_high.shape[0], to_low.shape[0])
        grow = lambda a: jnp.pad(a, ((0, size - a.shape[0]),) + ((0, 0),) * (a.ndim - 1))
        low, high = swap_halos(grow(to_high), grow(to_low), axis)
        halos += [low[: to_high.shape[0]], high[: to_low.shape[0]]]

    def widen(halo, keep):
        parts = [jnp.zeros_like(halo[vectors : vectors + 1])] * fields.shape[0]
        for place, index in enumerate(keep):
            parts[index] = halo[vectors + place : vectors + place + 1]
        return jnp.concatenate(parts)

    def assemble(block, low_x, high_x, low_y, high_y):
        block = jnp.concatenate([low_x, block, high_x], axis=1)
        edge = ((0, 0), (1, 1), (0, 0), (0, 0))
        return jnp.concatenate([jnp.pad(low_y, edge), block, jnp.pad(high_y, edge)], axis=2)

    fields_one = assemble(fields, *(widen(halo, keep) for halo, keep in zip(halos, sent)))
    together = assemble(field, *(halo[:vectors] for halo in halos))
    first = True
    for repeat in range(FILTER_STEPS):
        if first:
            applied = stencil(together, fields_one)
            first = False
        else:
            applied = operate(field, fields_one)
        middle = (applied - FILTER_CENTRE * field) / FILTER_HALF
        field = (
            2.0 * (operate(middle, fields_one) - FILTER_CENTRE * middle) / FILTER_HALF - field
        ) / FILTER_NORM
    flattened = field.reshape(vectors, -1)
    gram_sum = reduce_all(inner_products(flattened, flattened)) / cell_total
    inverse = triangle_inverse(gram_sum, vectors)
    basis_rows = combine(inverse, flattened)
    raw_images = operate(field, fields_one).reshape(vectors, -1)
    mixed_sum = reduce_all(inner_products(flattened, raw_images)) / cell_total
    projected = jnp.einsum(
        "ka,ab,lb->kl", inverse, mixed_sum, inverse, precision=lax.Precision.HIGHEST
    )
    residual = combine(inverse, raw_images) - combine(projected, basis_rows)
    return (basis_rows.reshape(field.shape), residual.reshape(field.shape))


def solution(mesh):
    placed = (
        P(None, "gx", "gy", None),
        P("gx", "gy", None),
        P("gx", "gy", None),
        P("gx", "gy", None),
        P("gx", "gy", None),
        P("gx", "gy", None),
    )
    return jax.shard_map(
        on_device,
        mesh=mesh,
        in_specs=placed,
        out_specs=(P(None, "gx", "gy", None), P(None, "gx", "gy", None)),
        check_vma=False,
    )
```

```python
import jax
import jax.numpy as jnp
from jax import lax
from jax.sharding import PartitionSpec as P

FILTER_STEPS = 2


FILTER_CENTRE = 22.0
FILTER_HALF = 18.0
FILTER_NORM = 2.0 * (22.0 / 18.0) * (22.0 / 18.0) - 1.0


def swap_halos(to_high, to_low, axis):
    count = lax.axis_size(axis)
    even = lax.axis_index(axis) % 2 == 0
    first = [(i, i ^ 1) for i in range(count - count % 2)]
    second = [(i, j) for i in range(1, count - 1) for j in (i + 1 if i % 2 else i - 1,)]
    got_first = lax.ppermute(jnp.where(even, to_high, to_low), axis, first)
    got_second = lax.ppermute(jnp.where(even, to_low, to_high), axis, second)
    low = jnp.where(even, got_second, got_first)
    high = jnp.where(even, got_first, got_second)
    return low, high


def halo_pair(block, axis, dim):
    return swap_halos(
        lax.slice_in_dim(block, block.shape[dim] - 1, None, axis=dim),
        lax.slice_in_dim(block, 0, 1, axis=dim),
        axis,
    )


def padded_2(block, sides, width):
    (axis_a, dim_a), (axis_b, dim_b) = sides
    low_a, high_a = halo_pair(block, axis_a, dim_a)
    low_b, high_b = halo_pair(block, axis_b, dim_b)
    block = jnp.concatenate([low_a, block, high_a], axis=dim_a)
    edge = [(0, 0)] * block.ndim
    edge[dim_a] = (1, 1)
    low_b = jnp.pad(low_b, edge)
    high_b = jnp.pad(high_b, edge)
    return jnp.concatenate([low_b, block, high_b], axis=dim_b)


def stencil(values, fields):
    wet_mask = fields[0]
    along_x = fields[1]
    along_y = fields[2]
    along_z = fields[3]
    diag_term = fields[4]
    inner_wet = wet_mask[1:-1, 1:-1]
    face_x = along_x[:-1, 1:-1] * wet_mask[:-1, 1:-1] * wet_mask[1:, 1:-1]
    flow_x = face_x * (values[..., 1:, 1:-1, :] - values[..., :-1, 1:-1, :])
    face_y = along_y[1:-1, :-1] * wet_mask[1:-1, :-1] * wet_mask[1:-1, 1:]
    flow_y = face_y * (values[..., 1:-1, 1:, :] - values[..., 1:-1, :-1, :])
    centre = values[..., 1:-1, 1:-1, :]
    face_z = along_z[1:-1, 1:-1, :-1] * inner_wet[:, :, :-1] * inner_wet[:, :, 1:]
    flow_z = face_z * (centre[..., 1:] - centre[..., :-1])
    edges = [(0, 0)] * (centre.ndim - 1)
    net_z = jnp.pad(flow_z, edges + [(1, 0)]) - jnp.pad(flow_z, edges + [(0, 1)])
    net_x = flow_x[..., :-1, :, :] - flow_x[..., 1:, :, :]
    net_y = flow_y[..., :-1, :] - flow_y[..., 1:, :]
    return inner_wet * (diag_term[1:-1, 1:-1] * centre + net_x + net_y + net_z)


def operate(block, fields_one):
    padded = padded_2(block, (("gx", 1), ("gy", 2)), 1)
    return stencil(padded, fields_one)


def reduce_all(value):
    for axis in ("gy", "gx"):
        count = lax.axis_size(axis)
        assert count & (count - 1) == 0
        step = 1
        while step < count:
            pairs = [(i, i ^ step) for i in range(count)]
            value = value + lax.ppermute(value, axis, pairs)
            step *= 2
    return value


def inner_products(left, right):
    return jnp.einsum("kc,lc->kl", left, right, precision=lax.Precision.HIGHEST)


def combine(matrix, rows):
    return jnp.einsum("kl,lc->kc", matrix, rows, precision=lax.Precision.HIGHEST)


def triangle_inverse(gram_sum, vectors):
    factor = jnp.linalg.cholesky(gram_sum)
    return lax.linalg.triangular_solve(
        factor, jnp.eye(vectors, dtype=jnp.float32), left_side=True, lower=True
    )


def on_device(start_panel, ocean_mask, conduct_x, conduct_y, conduct_z, diag_shift):
    ocean_cells = ocean_mask.astype(jnp.float32)
    vectors = start_panel.shape[0]
    cell_total = (
        start_panel.shape[1]
        * start_panel.shape[2]
        * start_panel.shape[3]
        * lax.axis_size("gx")
        * lax.axis_size("gy")
    )
    field = start_panel * ocean_cells[None]
    fields = jnp.stack([ocean_cells, conduct_x, conduct_y, conduct_z, diag_shift])
    rows, cols = field.shape[1], field.shape[2]
    sent = ((0, 1), (0,), (0, 2), (0,))
    edges = []
    for (dim, first), keep in zip(
        ((0, rows - 1), (0, 0), (1, cols - 1), (1, 0)), sent
    ):
        cut = lambda a, lead: lax.slice_in_dim(a, first, first + 1, axis=dim + lead)
        edges.append(
            jnp.concatenate([cut(field, 1), *(cut(fields[i : i + 1], 1) for i in keep)])
        )
    halos = []
    for axis, (to_high, to_low), (keep_high, keep_low) in (
        ("gx", edges[0:2], sent[0:2]),
        ("gy", edges[2:4], sent[2:4]),
    ):
        size = max(to_high.shape[0], to_low.shape[0])
        grow = lambda a: jnp.pad(a, ((0, size - a.shape[0]),) + ((0, 0),) * (a.ndim - 1))
        if halos:
            tie = 0.0 * (halos[0][0, 0, 0, 0] + halos[1][0, 0, 0, 0])
            to_high, to_low = to_high + tie, to_low + tie
        low, high = swap_halos(grow(to_high), grow(to_low), axis)
        halos += [low[: to_high.shape[0]], high[: to_low.shape[0]]]

    def widen(halo, keep):
        parts = [jnp.zeros_like(halo[vectors : vectors + 1])] * fields.shape[0]
        for place, index in enumerate(keep):
            parts[index] = halo[vectors + place : vectors + place + 1]
        return jnp.concatenate(parts)

    def assemble(block, low_x, high_x, low_y, high_y):
        block = jnp.concatenate([low_x, block, high_x], axis=1)
        edge = ((0, 0), (1, 1), (0, 0), (0, 0))
        return jnp.concatenate([jnp.pad(low_y, edge), block, jnp.pad(high_y, edge)], axis=2)

    fields_one = assemble(fields, *(widen(halo, keep) for halo, keep in zip(halos, sent)))
    together = assemble(field, *(halo[:vectors] for halo in halos))
    first = True
    for repeat in range(FILTER_STEPS):
        if first:
            applied = stencil(together, fields_one)
            first = False
        else:
            applied = operate(field, fields_one)
        middle = (applied - FILTER_CENTRE * field) / FILTER_HALF
        field = (
            2.0 * (operate(middle, fields_one) - FILTER_CENTRE * middle) / FILTER_HALF - field
        ) / FILTER_NORM
    flattened = field.reshape(vectors, -1)
    gram_sum = reduce_all(inner_products(flattened, flattened)) / cell_total
    inverse = triangle_inverse(gram_sum, vectors)
    basis_rows = combine(inverse, flattened)
    raw_images = operate(field, fields_one).reshape(vectors, -1)
    mixed_sum = reduce_all(inner_products(flattened, raw_images)) / cell_total
    projected = jnp.einsum(
        "ka,ab,lb->kl", inverse, mixed_sum, inverse, precision=lax.Precision.HIGHEST
    )
    residual = combine(inverse, raw_images) - combine(projected, basis_rows)
    return (basis_rows.reshape(field.shape), residual.reshape(field.shape))


def solution(mesh):
    placed = (
        P(None, "gx", "gy", None),
        P("gx", "gy", None),
        P("gx", "gy", None),
        P("gx", "gy", None),
        P("gx", "gy", None),
        P("gx", "gy", None),
    )
    return jax.shard_map(
        on_device,
        mesh=mesh,
        in_specs=placed,
        out_specs=(P(None, "gx", "gy", None), P(None, "gx", "gy", None)),
        check_vma=False,
    )
```

```python
import jax
import jax.numpy as jnp
from jax import lax
from jax.sharding import PartitionSpec as P

FILTER_STEPS = 2
CHAINS = 2


FILTER_CENTRE = 22.0
FILTER_HALF = 18.0
FILTER_NORM = 2.0 * (22.0 / 18.0) * (22.0 / 18.0) - 1.0


def swap_halos(to_high, to_low, axis):
    count = lax.axis_size(axis)
    even = lax.axis_index(axis) % 2 == 0
    first = [(i, i ^ 1) for i in range(count - count % 2)]
    second = [(i, j) for i in range(1, count - 1) for j in (i + 1 if i % 2 else i - 1,)]
    got_first = lax.ppermute(jnp.where(even, to_high, to_low), axis, first)
    got_second = lax.ppermute(jnp.where(even, to_low, to_high), axis, second)
    low = jnp.where(even, got_second, got_first)
    high = jnp.where(even, got_first, got_second)
    return low, high


def halo_pair(block, axis, dim):
    return swap_halos(
        lax.slice_in_dim(block, block.shape[dim] - 1, None, axis=dim),
        lax.slice_in_dim(block, 0, 1, axis=dim),
        axis,
    )


def padded_2(block, sides, width):
    (axis_a, dim_a), (axis_b, dim_b) = sides
    low_a, high_a = halo_pair(block, axis_a, dim_a)
    low_b, high_b = halo_pair(block, axis_b, dim_b)
    block = jnp.concatenate([low_a, block, high_a], axis=dim_a)
    edge = [(0, 0)] * block.ndim
    edge[dim_a] = (1, 1)
    low_b = jnp.pad(low_b, edge)
    high_b = jnp.pad(high_b, edge)
    return jnp.concatenate([low_b, block, high_b], axis=dim_b)


def stencil(values, fields):
    wet_mask = fields[0]
    along_x = fields[1]
    along_y = fields[2]
    along_z = fields[3]
    diag_term = fields[4]
    inner_wet = wet_mask[1:-1, 1:-1]
    face_x = along_x[:-1, 1:-1] * wet_mask[:-1, 1:-1] * wet_mask[1:, 1:-1]
    flow_x = face_x * (values[..., 1:, 1:-1, :] - values[..., :-1, 1:-1, :])
    face_y = along_y[1:-1, :-1] * wet_mask[1:-1, :-1] * wet_mask[1:-1, 1:]
    flow_y = face_y * (values[..., 1:-1, 1:, :] - values[..., 1:-1, :-1, :])
    centre = values[..., 1:-1, 1:-1, :]
    face_z = along_z[1:-1, 1:-1, :-1] * inner_wet[:, :, :-1] * inner_wet[:, :, 1:]
    flow_z = face_z * (centre[..., 1:] - centre[..., :-1])
    edges = [(0, 0)] * (centre.ndim - 1)
    net_z = jnp.pad(flow_z, edges + [(1, 0)]) - jnp.pad(flow_z, edges + [(0, 1)])
    net_x = flow_x[..., :-1, :, :] - flow_x[..., 1:, :, :]
    net_y = flow_y[..., :-1, :] - flow_y[..., 1:, :]
    return inner_wet * (diag_term[1:-1, 1:-1] * centre + net_x + net_y + net_z)


def operate(block, fields_one):
    padded = padded_2(block, (("gx", 1), ("gy", 2)), 1)
    return stencil(padded, fields_one)


def reduce_all(value):
    for axis in ("gy", "gx"):
        count = lax.axis_size(axis)
        assert count & (count - 1) == 0
        step = 1
        while step < count:
            pairs = [(i, i ^ step) for i in range(count)]
            value = value + lax.ppermute(value, axis, pairs)
            step *= 2
    return value


def inner_products(left, right):
    return jnp.einsum("kc,lc->kl", left, right, precision=lax.Precision.HIGHEST)


def combine(matrix, rows):
    return jnp.einsum("kl,lc->kc", matrix, rows, precision=lax.Precision.HIGHEST)


def triangle_inverse(gram_sum, vectors):
    factor = jnp.linalg.cholesky(gram_sum)
    return lax.linalg.triangular_solve(
        factor, jnp.eye(vectors, dtype=jnp.float32), left_side=True, lower=True
    )


def on_device(start_panel, ocean_mask, conduct_x, conduct_y, conduct_z, diag_shift):
    ocean_cells = ocean_mask.astype(jnp.float32)
    vectors = start_panel.shape[0]
    cell_total = (
        start_panel.shape[1]
        * start_panel.shape[2]
        * start_panel.shape[3]
        * lax.axis_size("gx")
        * lax.axis_size("gy")
    )
    field = start_panel * ocean_cells[None]
    fields = jnp.stack([ocean_cells, conduct_x, conduct_y, conduct_z, diag_shift])
    rows, cols = field.shape[1], field.shape[2]
    sent = ((0, 1), (0,), (0, 2), (0,))
    edges = []
    for (dim, first), keep in zip(
        ((0, rows - 1), (0, 0), (1, cols - 1), (1, 0)), sent
    ):
        cut = lambda a, lead: lax.slice_in_dim(a, first, first + 1, axis=dim + lead)
        edges.append(
            jnp.concatenate([cut(field, 1), *(cut(fields[i : i + 1], 1) for i in keep)])
        )
    halos = []
    for axis, (to_high, to_low), (keep_high, keep_low) in (
        ("gx", edges[0:2], sent[0:2]),
        ("gy", edges[2:4], sent[2:4]),
    ):
        size = max(to_high.shape[0], to_low.shape[0])
        grow = lambda a: jnp.pad(a, ((0, size - a.shape[0]),) + ((0, 0),) * (a.ndim - 1))
        low, high = swap_halos(grow(to_high), grow(to_low), axis)
        halos += [low[: to_high.shape[0]], high[: to_low.shape[0]]]

    def widen(halo, keep):
        parts = [jnp.zeros_like(halo[vectors : vectors + 1])] * fields.shape[0]
        for place, index in enumerate(keep):
            parts[index] = halo[vectors + place : vectors + place + 1]
        return jnp.concatenate(parts)

    def assemble(block, low_x, high_x, low_y, high_y):
        block = jnp.concatenate([low_x, block, high_x], axis=1)
        edge = ((0, 0), (1, 1), (0, 0), (0, 0))
        return jnp.concatenate([jnp.pad(low_y, edge), block, jnp.pad(high_y, edge)], axis=2)

    fields_one = assemble(fields, *(widen(halo, keep) for halo, keep in zip(halos, sent)))
    together = assemble(field, *(halo[:vectors] for halo in halos))
    applied = stencil(together, fields_one)
    share = vectors // CHAINS
    finished = []
    for chain in range(CHAINS):
        part = slice(chain * share, (chain + 1) * share)
        field_part = field[part]
        applied_part = applied[part]
        for repeat in range(FILTER_STEPS):
            if repeat:
                applied_part = operate(field_part, fields_one)
            middle = (applied_part - FILTER_CENTRE * field_part) / FILTER_HALF
            field_part = (
                2.0 * (operate(middle, fields_one) - FILTER_CENTRE * middle) / FILTER_HALF
                - field_part
            ) / FILTER_NORM
        finished.append(field_part)
    field = jnp.concatenate(finished)
    flattened = field.reshape(vectors, -1)
    gram_sum = reduce_all(inner_products(flattened, flattened)) / cell_total
    inverse = triangle_inverse(gram_sum, vectors)
    basis_rows = combine(inverse, flattened)
    raw_images = operate(field, fields_one).reshape(vectors, -1)
    mixed_sum = reduce_all(inner_products(flattened, raw_images)) / cell_total
    projected = jnp.einsum(
        "ka,ab,lb->kl", inverse, mixed_sum, inverse, precision=lax.Precision.HIGHEST
    )
    residual = combine(inverse, raw_images) - combine(projected, basis_rows)
    return (basis_rows.reshape(field.shape), residual.reshape(field.shape))


def solution(mesh):
    placed = (
        P(None, "gx", "gy", None),
        P("gx", "gy", None),
        P("gx", "gy", None),
        P("gx", "gy", None),
        P("gx", "gy", None),
        P("gx", "gy", None),
    )
    return jax.shard_map(
        on_device,
        mesh=mesh,
        in_specs=placed,
        out_specs=(P(None, "gx", "gy", None), P(None, "gx", "gy", None)),
        check_vma=False,
    )
```

```python
import jax
import jax.numpy as jnp
from jax import lax
from jax.sharding import PartitionSpec as P

FILTER_STEPS = 2


FILTER_CENTRE = 22.0
FILTER_HALF = 18.0
FILTER_NORM = 2.0 * (22.0 / 18.0) * (22.0 / 18.0) - 1.0


def swap_halos(to_high, to_low, axis):
    count = lax.axis_size(axis)
    even = lax.axis_index(axis) % 2 == 0
    first = [(i, i ^ 1) for i in range(count - count % 2)]
    second = [(i, j) for i in range(1, count - 1) for j in (i + 1 if i % 2 else i - 1,)]
    got_first = lax.ppermute(jnp.where(even, to_high, to_low), axis, first)
    got_second = lax.ppermute(jnp.where(even, to_low, to_high), axis, second)
    low = jnp.where(even, got_second, got_first)
    high = jnp.where(even, got_first, got_second)
    return low, high


def halo_pair(block, axis, dim):
    return swap_halos(
        lax.slice_in_dim(block, block.shape[dim] - 1, None, axis=dim),
        lax.slice_in_dim(block, 0, 1, axis=dim),
        axis,
    )


def padded_2(block, sides, width):
    (axis_a, dim_a), (axis_b, dim_b) = sides
    low_a, high_a = halo_pair(block, axis_a, dim_a)
    low_b, high_b = halo_pair(block, axis_b, dim_b)
    block = jnp.concatenate([low_a, block, high_a], axis=dim_a)
    edge = [(0, 0)] * block.ndim
    edge[dim_a] = (1, 1)
    low_b = jnp.pad(low_b, edge)
    high_b = jnp.pad(high_b, edge)
    return jnp.concatenate([low_b, block, high_b], axis=dim_b)


def stencil(values, fields):
    wet_mask = fields[0]
    along_x = fields[1]
    along_y = fields[2]
    along_z = fields[3]
    diag_term = fields[4]
    inner_wet = wet_mask[1:-1, 1:-1]
    face_x = along_x[:-1, 1:-1] * wet_mask[:-1, 1:-1] * wet_mask[1:, 1:-1]
    flow_x = face_x * (values[..., 1:, 1:-1, :] - values[..., :-1, 1:-1, :])
    face_y = along_y[1:-1, :-1] * wet_mask[1:-1, :-1] * wet_mask[1:-1, 1:]
    flow_y = face_y * (values[..., 1:-1, 1:, :] - values[..., 1:-1, :-1, :])
    centre = values[..., 1:-1, 1:-1, :]
    face_z = along_z[1:-1, 1:-1, :-1] * inner_wet[:, :, :-1] * inner_wet[:, :, 1:]
    flow_z = face_z * (centre[..., 1:] - centre[..., :-1])
    edges = [(0, 0)] * (centre.ndim - 1)
    net_z = jnp.pad(flow_z, edges + [(1, 0)]) - jnp.pad(flow_z, edges + [(0, 1)])
    net_x = flow_x[..., :-1, :, :] - flow_x[..., 1:, :, :]
    net_y = flow_y[..., :-1, :] - flow_y[..., 1:, :]
    return inner_wet * (diag_term[1:-1, 1:-1] * centre + net_x + net_y + net_z)


def operate(block, fields_one):
    padded = padded_2(block, (("gx", 1), ("gy", 2)), 1)
    return stencil(padded, fields_one)


def reduce_all(value):
    for axis in ("gx", "gy"):
        count = lax.axis_size(axis)
        assert count & (count - 1) == 0
        step = 1
        while step < count:
            pairs = [(i, i ^ step) for i in range(count)]
            value = value + lax.ppermute(value, axis, pairs)
            step *= 2
    return value


def inner_products(left, right):
    return jnp.einsum("kc,lc->kl", left, right, precision=lax.Precision.HIGHEST)


def combine(matrix, rows):
    return jnp.einsum("kl,lc->kc", matrix, rows, precision=lax.Precision.HIGHEST)


def triangle_inverse(gram_sum, vectors):
    factor = jnp.linalg.cholesky(gram_sum)
    return lax.linalg.triangular_solve(
        factor, jnp.eye(vectors, dtype=jnp.float32), left_side=True, lower=True
    )


def on_device(start_panel, ocean_mask, conduct_x, conduct_y, conduct_z, diag_shift):
    ocean_cells = ocean_mask.astype(jnp.float32)
    vectors = start_panel.shape[0]
    cell_total = (
        start_panel.shape[1]
        * start_panel.shape[2]
        * start_panel.shape[3]
        * lax.axis_size("gx")
        * lax.axis_size("gy")
    )
    field = start_panel * ocean_cells[None]
    fields = jnp.stack([ocean_cells, conduct_x, conduct_y, conduct_z, diag_shift])
    rows, cols = field.shape[1], field.shape[2]
    sent = ((0, 1), (0,), (0, 2), (0,))
    edges = []
    for (dim, first), keep in zip(
        ((0, rows - 1), (0, 0), (1, cols - 1), (1, 0)), sent
    ):
        cut = lambda a, lead: lax.slice_in_dim(a, first, first + 1, axis=dim + lead)
        edges.append(
            jnp.concatenate([cut(field, 1), *(cut(fields[i : i + 1], 1) for i in keep)])
        )
    halos = []
    for axis, (to_high, to_low), (keep_high, keep_low) in (
        ("gx", edges[0:2], sent[0:2]),
        ("gy", edges[2:4], sent[2:4]),
    ):
        size = max(to_high.shape[0], to_low.shape[0])
        grow = lambda a: jnp.pad(a, ((0, size - a.shape[0]),) + ((0, 0),) * (a.ndim - 1))
        low, high = swap_halos(grow(to_high), grow(to_low), axis)
        halos += [low[: to_high.shape[0]], high[: to_low.shape[0]]]

    def widen(halo, keep):
        parts = [jnp.zeros_like(halo[vectors : vectors + 1])] * fields.shape[0]
        for place, index in enumerate(keep):
            parts[index] = halo[vectors + place : vectors + place + 1]
        return jnp.concatenate(parts)

    def assemble(block, low_x, high_x, low_y, high_y):
        block = jnp.concatenate([low_x, block, high_x], axis=1)
        edge = ((0, 0), (1, 1), (0, 0), (0, 0))
        return jnp.concatenate([jnp.pad(low_y, edge), block, jnp.pad(high_y, edge)], axis=2)

    fields_one = assemble(fields, *(widen(halo, keep) for halo, keep in zip(halos, sent)))
    together = assemble(field, *(halo[:vectors] for halo in halos))
    first = True
    for repeat in range(FILTER_STEPS):
        if first:
            applied = stencil(together, fields_one)
            first = False
        else:
            applied = operate(field, fields_one)
        middle = (applied - FILTER_CENTRE * field) / FILTER_HALF
        field = (
            2.0 * (operate(middle, fields_one) - FILTER_CENTRE * middle) / FILTER_HALF - field
        ) / FILTER_NORM
    flattened = field.reshape(vectors, -1)
    gram_sum = reduce_all(inner_products(flattened, flattened)) / cell_total
    inverse = triangle_inverse(gram_sum, vectors)
    basis_rows = combine(inverse, flattened)
    raw_images = operate(field, fields_one).reshape(vectors, -1)
    mixed_sum = reduce_all(inner_products(flattened, raw_images)) / cell_total
    projected = jnp.einsum(
        "ka,ab,lb->kl", inverse, mixed_sum, inverse, precision=lax.Precision.HIGHEST
    )
    residual = combine(inverse, raw_images) - combine(projected, basis_rows)
    return (basis_rows.reshape(field.shape), residual.reshape(field.shape))


def solution(mesh):
    placed = (
        P(None, "gx", "gy", None),
        P("gx", "gy", None),
        P("gx", "gy", None),
        P("gx", "gy", None),
        P("gx", "gy", None),
        P("gx", "gy", None),
    )
    return jax.shard_map(
        on_device,
        mesh=mesh,
        in_specs=placed,
        out_specs=(P(None, "gx", "gy", None), P(None, "gx", "gy", None)),
        check_vma=False,
    )
```
